128 devices in a mesh: tile: 32 (over x_lo, y, z), src: 4 (over x_hi, core).
Axes of the slice: x: 4 (x_hi: 2, x_lo: 2; x = x_hi * 2 + x_lo), y: 4, z: 4, core: 2. Of those that a mesh axis runs over, the one named last changes fastest.
Arguments:
- tile_tokens: bfloat16 [32768, 2048], P(('tile', 'src')), may hold values from -6 to 6
- norm_gain: float32 [2048], replicated, may hold values from 0.25 to 2.5
- up_weight: bfloat16 [2048, 2816], P('tile'), may hold values from -0.125 to 0.125
- down_weight: bfloat16 [2816, 2048], P('tile'), may hold values from -0.109375 to 0.109375
- head_weight: bfloat16 [2048, 768], P(None, 'src'), may hold values from -0.125 to 0.125
- source_index: int32 [128, 2], replicated, may hold values from 0 to 96, as said below
- source_cutoff: int32 [128], replicated, may hold values from 8 to 16
- source_weight: float32 [128], replicated, may hold values from 0.3 to 3
Outputs:
- intensity: float32 [128, 4096], P(('tile', 'src'))
The draws below stay inside these ranges and needn't reach their ends.
Inputs may be any that keep to these rules, and one draw needn't show every extreme that they name: `source_index`: in each aligned group of 4 source points the first has the least value of the group in both coordinates, the second lies exactly 32 beyond it in both, and every other lies within 32 of the first in both.
All inputs are finite; a program needn't handle non-finite values.
Results may differ from the reference program's by a relative error of at most 0.0007.
Values may be sent and summed in bfloat16 or wider, within the bound.
No kernel may reach another device: no remote copies, remote signals or barrier semaphores. Data moves between devices by JAX's collectives and lax.ppermute only.
A program may use at most 128 MiB of HBM per device.

```python
import math
import jax
import jax.numpy as jnp
from jax import lax

D = 2048
FF = 2816
GRID = 16
SUB = 8
W = 32
REG = 64
PIX = 64
SRC_DEV = 4
PATCH = 256
ORD = 128
HEADW = 768
TOKENS = 32768
SOURCES = 128


def draw_source_index(key, part):
    group_count = SOURCES // SRC_DEV
    key_one, key_two, key_three, key_four = jax.random.split(key, 4)
    anchor = jax.random.randint(key_one, (group_count, 2), 0, ORD - REG + 1)
    top_group = jax.random.randint(key_two, (2,), 0, group_count)
    low_group = (top_group + 1 + jax.random.randint(key_three, (2,), 0, max(group_count - 1, 1))) % group_count
    group_rows = jnp.arange(group_count, dtype=jnp.int32)[:, None]
    anchor = jnp.where(group_rows == top_group[None, :], ORD - REG, anchor)
    anchor = jnp.where(group_rows == low_group[None, :], 0, anchor)
    span_width = REG - W
    offsets = jax.random.randint(key_four, (group_count, SRC_DEV, 2), 0, span_width + 1)
    member = jnp.arange(SRC_DEV, dtype=jnp.int32)[None, :, None]
    offsets = jnp.where(member == 0, 0, jnp.where(member == 1, span_width, offsets))
    return (anchor[:, None, :] + offsets).reshape(SOURCES, 2).astype(jnp.int32)


def plant(result, rng, least, largest):
    index_at = [jax.random.randint(jax.random.fold_in(rng, axis), (), 0, length) for axis, length in enumerate(result.shape)]
    main_axis = result.shape.index(max(result.shape))
    next_to = index_at[:main_axis] + [(index_at[main_axis] + 1) % result.shape[main_axis]] + index_at[main_axis + 1:]
    return result.at[tuple(index_at)].set(least).at[tuple(next_to)].set(largest)


def block_levels(own_key, dims, cuts, least, top_value):
    def one(axis_at, shards_of):
        steps = jax.random.uniform(jax.random.fold_in(jax.random.fold_in(own_key, 6), axis_at), (shards_of,), jnp.float32, least / len(cuts), top_value / len(cuts))
        return jnp.repeat(jnp.exp(steps), dims[axis_at] // shards_of).reshape((-1,) + (1,) * (len(dims) - axis_at - 1))

    factor_of = one(*cuts[0])
    for cut in cuts[1:]:
        factor_of = factor_of * one(*cut)
    return factor_of


def gaussian(key, dims, scale, most, shards=(), kind=jnp.bfloat16):
    values = scale * jax.random.normal(key, dims, jnp.float32)
    if shards:
        values = values * block_levels(key, dims, shards, -0.22, 0.18)
    return jnp.clip(values, -most, most).astype(kind)


def setup_inputs(seed: int = 0) -> dict:
    arg_keys = jax.random.split(jax.random.key(seed), 9)
    tile_tokens = gaussian(arg_keys[0], (TOKENS, D), 1.0, 6.0, ((0, 128),))
    norm_gain = jnp.clip(jnp.exp(jax.random.uniform(arg_keys[1], (D,), jnp.float32, math.log(0.25), math.log(2.5))), 0.25, 2.5)
    up_weight = gaussian(arg_keys[2], (D, FF), D ** -0.5, 0.125, ((0, 32),))
    down_weight = gaussian(arg_keys[3], (FF, D), FF ** -0.5, 0.109375, ((0, 32),))
    head_weight = gaussian(arg_keys[4], (D, HEADW), D ** -0.5, 0.125, ((1, 4),))
    source_index = draw_source_index(jax.random.fold_in(arg_keys[8], 71), 0)
    source_cutoff = plant(jax.random.randint(arg_keys[6], (SOURCES,), W // 4, W // 2 + 1), jax.random.fold_in(arg_keys[6], 1), W // 4, (W // 2 + 1) - 1).astype(jnp.int32)
    source_weight = jnp.clip(jnp.exp(jax.random.uniform(arg_keys[7], (SOURCES,), jnp.float32, math.log(0.3), math.log(3.0))), 0.3, 3.0)
    return dict(tile_tokens=tile_tokens, norm_gain=norm_gain, up_weight=up_weight, down_weight=down_weight, head_weight=head_weight, source_index=source_index, source_cutoff=source_cutoff, source_weight=source_weight)


def dft_tables():
    frequency = jnp.arange(W, dtype=jnp.int32) - W // 2
    position = jnp.arange(PIX, dtype=jnp.int32)
    phase_turns = jnp.mod(frequency[:, None] * position[None, :], PIX).astype(jnp.float32)
    phase_angle = phase_turns * (2.0 * math.pi / PIX)
    cosine = jnp.cos(phase_angle)
    sine_table = jnp.sin(phase_angle)
    table_one = jnp.concatenate([jnp.concatenate([cosine, sine_table], 1), jnp.concatenate([-sine_table, cosine], 1)], 0)
    table_two = jnp.concatenate([jnp.concatenate([cosine.T, -sine_table.T], 1), jnp.concatenate([sine_table.T, cosine.T], 1)], 0)
    return (table_one, table_two)

def pupil_mask(radius):
    frequency = jnp.arange(W, dtype=jnp.int32) - W // 2
    distance = frequency[:, None] * frequency[:, None] + frequency[None, :] * frequency[None, :]
    return (distance <= radius * radius).astype(jnp.bfloat16)

def source_power(window, table_one, table_two):
    tile_count = window.shape[0]
    split_parts = window.reshape(tile_count, 6, 2, W, W).transpose(0, 1, 3, 2, 4).reshape(tile_count, 6, W, 2 * W)
    half_field = jnp.einsum('bcik,ky->bciy', split_parts.astype(jnp.float32), table_one, precision=lax.Precision.HIGHEST)
    half_field = half_field.reshape(tile_count, 6, W, 2, PIX).transpose(0, 1, 3, 2, 4).reshape(tile_count, 6, 2 * W, PIX)
    image_field = jnp.einsum('pk,bcky->bcpy', table_two, half_field, precision=lax.Precision.HIGHEST)
    power_map = lax.optimization_barrier(jnp.sum((image_field * image_field).reshape(tile_count, 12, PIX, PIX), axis=1))
    return power_map.reshape(tile_count, PIX * PIX)

def surrogate(token_rows, norm_gain, up_weight, down_weight, head_weight):
    residual = token_rows.astype(jnp.float32)
    mean_square = lax.optimization_barrier(jnp.mean(residual * residual, axis=1, keepdims=True))
    normed = (residual * lax.rsqrt(mean_square + 1e-05) * norm_gain).astype(jnp.bfloat16)
    hidden = jax.nn.gelu(jnp.dot(normed, up_weight, preferred_element_type=jnp.float32)).astype(jnp.bfloat16)
    mixed = (residual + jnp.dot(hidden, down_weight, preferred_element_type=jnp.float32)).astype(jnp.bfloat16)
    return jnp.dot(mixed, head_weight, preferred_element_type=jnp.float32).astype(jnp.bfloat16)

def reference(tile_tokens, norm_gain, up_weight, down_weight, head_weight, source_index, source_cutoff, source_weight):
    tile_count = tile_tokens.shape[0] // PATCH

    def one_tile(token_rows):
        return surrogate(token_rows, norm_gain, up_weight, down_weight, head_weight)
    coeffs = lax.map(one_tile, tile_tokens.reshape(tile_count, PATCH, D))
    spectra = coeffs.reshape(tile_count, GRID, GRID, 12, SUB, SUB).transpose(0, 3, 1, 4, 2, 5).reshape(tile_count, 12, ORD, ORD)
    table_one, table_two = dft_tables()
    anchor_zero = jnp.zeros((), jnp.int32)

    def add_source(running, source_item):
        corner_at, radius, weight = source_item
        corner_at = corner_at.astype(jnp.int32)
        window = lax.dynamic_slice(spectra, (anchor_zero, anchor_zero, corner_at[0], corner_at[1]), (tile_count, 12, W, W)) * pupil_mask(radius)
        return (running + weight * source_power(window, table_one, table_two), None)
    running = jnp.zeros((tile_count, PIX * PIX), jnp.float32)
    image_sum, unused = lax.scan(add_source, running, (source_index, source_cutoff, source_weight))
    return image_sum * (1.0 / (6.0 * W * W * source_weight.shape[0]))
```

```python
import math

import jax
import jax.numpy as jnp
from jax import lax
from jax.sharding import PartitionSpec as P

GRID = 16
SUB = 8
W = 32
REG = 64
PIX = 64
SRC_DEV = 4
PATCH = 256
ORD = 128
f32 = jnp.float32
bf16 = jnp.bfloat16


def split_bf16(x):
    hi = lax.reduce_precision(x, exponent_bits=8, mantissa_bits=7)
    lo = x - hi
    return hi.astype(bf16), lo.astype(bf16)


def phase_tables():
    turn = 2.0 * math.pi / PIX
    v = jnp.arange(ORD, dtype=jnp.int32)
    y = jnp.arange(PIX, dtype=jnp.int32)
    ang = jnp.mod(v[:, None] * y[None, :], PIX).astype(f32) * turn
    cv, sv = jnp.cos(ang), jnp.sin(ang)
    t1 = jnp.stack([jnp.concatenate([cv, sv], 1), jnp.concatenate([-sv, cv], 1)], 0)
    i = jnp.arange(W, dtype=jnp.int32)
    x = jnp.arange(PIX, dtype=jnp.int32)
    ang2 = jnp.mod(x[:, None] * i[None, :], PIX).astype(f32) * turn
    ca, sa = jnp.cos(ang2), jnp.sin(ang2)
    t2 = jnp.stack([jnp.stack([ca, -sa], 1), jnp.stack([sa, ca], 1)], 0)
    return t1, t2


def imaging(spec, source_index, source_cutoff, source_weight):
    T = spec.shape[0]
    S = source_index.shape[0]
    x0 = jnp.clip(source_index[:, 0], 0, ORD - W)
    y0 = jnp.clip(source_index[:, 1], 0, ORD - W)
    rows = (x0[:, None] + jnp.arange(W, dtype=jnp.int32)[None, :]).reshape(-1)
    spec_rows = spec.reshape(T, 6, 2, ORD, ORD).transpose(3, 0, 1, 2, 4)
    strips = jnp.take(spec_rows, rows, axis=0, mode="clip").reshape(S, W, T, 6, 2, ORD)
    i = jnp.arange(W, dtype=jnp.int32)
    j = jnp.arange(ORD, dtype=jnp.int32)[None, :] - y0[:, None]
    dist = (i[None, :, None] - W // 2) ** 2 + (j[:, None, :] - W // 2) ** 2
    keep = (dist <= (source_cutoff * source_cutoff)[:, None, None]) & (j[:, None, :] >= 0) & (j[:, None, :] < W)
    masked = jnp.where(keep[:, :, None, None, None, :], strips, jnp.zeros((), bf16))
    t1, t2 = phase_tables()
    t1h, t1l = split_bf16(t1)
    t1s = jnp.concatenate([t1h, t1l], -1)
    out1 = jnp.einsum("sitkpv,pvn->sitkn", masked, t1s, preferred_element_type=f32)
    half = out1[..., : 2 * PIX] + out1[..., 2 * PIX:]
    half = half.reshape(S, W, T, 6, 2, PIX)
    hh, hl = split_bf16(half)
    hcat = jnp.concatenate([hh, hl, hh], 4)
    t2h, t2l = split_bf16(t2)
    t2cat = jnp.concatenate([t2h, t2h, t2l], 2)
    field = jnp.einsum("cxqi,sitkqy->tskcxy", t2cat, hcat, preferred_element_type=f32)
    power = jnp.sum(field * field * source_weight[None, :, None, None, None, None], axis=(1, 2, 3))
    return power.reshape(T, PIX * PIX) * (1.0 / (6.0 * W * W * S))


def local(
    tile_tokens,
    norm_gain,
    up_weight,
    down_weight,
    head_weight,
    source_index,
    source_cutoff,
    source_weight,
):
    residual = tile_tokens.astype(jnp.float32)
    mean_square = jnp.mean(residual * residual, axis=1, keepdims=True)
    normed = (residual * lax.rsqrt(mean_square + 1e-05) * norm_gain).astype(jnp.bfloat16)
    token_count = tile_tokens.shape[0]
    columns = normed
    pre_act = jnp.dot(
        columns,
        lax.all_gather(up_weight, "tile", axis=0, tiled=True),
        preferred_element_type=jnp.float32,
    )
    hidden = jax.nn.gelu(pre_act).astype(jnp.bfloat16)
    columns = hidden
    branch_out = jnp.dot(
        columns,
        lax.all_gather(down_weight, "tile", axis=0, tiled=True),
        preferred_element_type=jnp.float32,
    )
    mixed = (residual + branch_out).astype(jnp.bfloat16)
    coeffs = jnp.dot(
        mixed,
        lax.all_gather(head_weight, "src", axis=1, tiled=True),
        preferred_element_type=jnp.float32,
    ).astype(jnp.bfloat16)
    tile_count = token_count // PATCH
    spectra = (
        coeffs.reshape(tile_count, GRID, GRID, 12, SUB, SUB)
        .transpose(0, 3, 1, 4, 2, 5)
        .reshape(tile_count, 12, ORD, ORD)
    )
    return imaging(spectra, source_index, source_cutoff, source_weight)


def solution(mesh):
    return jax.shard_map(
        local,
        mesh=mesh,
        in_specs=(
            P(("tile", "src"), None),
            P(),
            P("tile", None),
            P("tile", None),
            P(None, "src"),
            P(),
            P(),
            P(),
        ),
        out_specs=P(("tile", "src"), None),
        check_vma=False,
    )
```

```python
import math

import jax
import jax.numpy as jnp
from jax import lax
from jax.sharding import PartitionSpec as P

GRID = 16
SUB = 8
W = 32
REG = 64
PIX = 64
SRC_DEV = 4
PATCH = 256
ORD = 128
f32 = jnp.float32
bf16 = jnp.bfloat16


def split_bf16(x):
    hi = lax.reduce_precision(x, exponent_bits=8, mantissa_bits=7)
    lo = x - hi
    return hi.astype(bf16), lo.astype(bf16)


def phase_tables():
    turn = 2.0 * math.pi / PIX
    v = jnp.arange(ORD, dtype=jnp.int32)
    y = jnp.arange(PIX, dtype=jnp.int32)
    ang = jnp.mod(v[:, None] * y[None, :], PIX).astype(f32) * turn
    cv, sv = jnp.cos(ang), jnp.sin(ang)
    t1 = jnp.stack([jnp.concatenate([cv, sv], 1), jnp.concatenate([-sv, cv], 1)], 0)
    i = jnp.arange(W, dtype=jnp.int32)
    x = jnp.arange(PIX, dtype=jnp.int32)
    ang2 = jnp.mod(x[:, None] * i[None, :], PIX).astype(f32) * turn
    ca, sa = jnp.cos(ang2), jnp.sin(ang2)
    t2 = jnp.stack([jnp.stack([ca, -sa], 1), jnp.stack([sa, ca], 1)], 0)
    return t1, t2


def imaging(spec, source_index, source_cutoff, source_weight):
    T = spec.shape[0]
    S = source_index.shape[0]
    x0 = jnp.clip(source_index[:, 0], 0, ORD - W)
    y0 = jnp.clip(source_index[:, 1], 0, ORD - W)
    rows = (x0[:, None] + jnp.arange(W, dtype=jnp.int32)[None, :]).reshape(-1)
    spec_rows = spec.reshape(T, 6, 2, ORD, ORD).transpose(3, 0, 1, 2, 4)
    strips = jnp.take(spec_rows, rows, axis=0, mode="clip").reshape(S, W, T, 6, 2, ORD)
    i = jnp.arange(W, dtype=jnp.int32)
    j = jnp.arange(ORD, dtype=jnp.int32)[None, :] - y0[:, None]
    dist = (i[None, :, None] - W // 2) ** 2 + (j[:, None, :] - W // 2) ** 2
    keep = (dist <= (source_cutoff * source_cutoff)[:, None, None]) & (j[:, None, :] >= 0) & (j[:, None, :] < W)
    masked = jnp.where(keep[:, :, None, None, None, :], strips, jnp.zeros((), bf16))
    t1, t2 = phase_tables()
    t1h, t1l = split_bf16(t1)
    t1s = jnp.concatenate([t1h, t1l], -1)
    out1 = jnp.einsum("sitkpv,pvn->sitkn", masked, t1s, preferred_element_type=f32)
    half = out1[..., : 2 * PIX] + out1[..., 2 * PIX:]
    half = half.reshape(S, W, T, 6, 2, PIX)
    hh, hl = split_bf16(half)
    hcat = jnp.concatenate([hh, hl, hh], 4)
    t2h, t2l = split_bf16(t2)
    t2cat = jnp.concatenate([t2h, t2h, t2l], 2)
    field = jnp.einsum("cxqi,sitkqy->tskcxy", t2cat, hcat, preferred_element_type=f32)
    power = jnp.sum(field * field * source_weight[None, :, None, None, None, None], axis=(1, 2, 3))
    return power.reshape(T, PIX * PIX) * (1.0 / (6.0 * W * W * S))


def local(
    tile_tokens,
    norm_gain,
    up_weight,
    down_weight,
    head_weight,
    source_index,
    source_cutoff,
    source_weight,
):
    token_count, d_model = tile_tokens.shape
    n_tile = lax.axis_size("tile")
    n_src = lax.axis_size("src")
    me = lax.axis_index("src")
    half = me % 2
    up_rows, ff = up_weight.shape
    down_rows = down_weight.shape[0]
    up_part = lax.dynamic_slice_in_dim(up_weight, half * (up_rows // 2), up_rows // 2, 0)
    down_part = lax.dynamic_slice_in_dim(down_weight, half * (down_rows // 2), down_rows // 2, 0)
    packed = jnp.concatenate([up_part, down_part.reshape(-1, ff)], 0)
    gathered = lax.all_gather(packed, "tile", axis=0, tiled=False)
    sibling = lax.ppermute(gathered, "src", [(s, s ^ 1) for s in range(n_src)])
    head_parts = [head_weight] + [
        lax.ppermute(head_weight, "src", [(s, s ^ k) for s in range(n_src)]) for k in range(1, n_src)
    ]

    residual = tile_tokens.astype(jnp.float32)
    mean_square = jnp.mean(residual * residual, axis=1, keepdims=True)
    normed = (residual * lax.rsqrt(mean_square + 1e-05) * norm_gain).astype(jnp.bfloat16)

    def halves(x, rows):
        view = x.reshape(x.shape[0], n_tile, 2, rows // 2)
        mine = lax.dynamic_index_in_dim(view, half, 2, keepdims=False)
        other = lax.dynamic_index_in_dim(view, 1 - half, 2, keepdims=False)
        return mine.reshape(x.shape[0], -1), other.reshape(x.shape[0], -1)

    def weights(g):
        up_w = g[:, : up_rows // 2, :].reshape(-1, ff)
        down_w = g[:, up_rows // 2:, :].reshape(n_tile * (down_rows // 2), d_model)
        return up_w, down_w

    up_mine, down_mine = weights(gathered)
    up_other, down_other = weights(sibling)
    normed_mine, normed_other = halves(normed, up_rows)
    pre_act = jnp.dot(normed_mine, up_mine, preferred_element_type=jnp.float32) + jnp.dot(
        normed_other, up_other, preferred_element_type=jnp.float32
    )
    hidden = jax.nn.gelu(pre_act).astype(jnp.bfloat16)
    hidden_mine, hidden_other = halves(hidden, down_rows)
    branch_out = jnp.dot(hidden_mine, down_mine, preferred_element_type=jnp.float32) + jnp.dot(
        hidden_other, down_other, preferred_element_type=jnp.float32
    )
    mixed = (residual + branch_out).astype(jnp.bfloat16)
    parts = jnp.stack(head_parts, 0)
    coeff_parts = jnp.einsum("tk,pkc->ptc", mixed, parts, preferred_element_type=jnp.float32).astype(
        jnp.bfloat16
    )
    order = me ^ jnp.arange(n_src, dtype=jnp.int32)
    coeffs = jnp.take(coeff_parts, order, axis=0).transpose(1, 0, 2).reshape(token_count, -1)
    tile_count = token_count // PATCH
    spectra = (
        coeffs.reshape(tile_count, GRID, GRID, 12, SUB, SUB)
        .transpose(0, 3, 1, 4, 2, 5)
        .reshape(tile_count, 12, ORD, ORD)
    )
    return imaging(spectra, source_index, source_cutoff, source_weight)


def solution(mesh):
    return jax.shard_map(
        local,
        mesh=mesh,
        in_specs=(
            P(("tile", "src"), None),
            P(),
            P("tile", None),
            P("tile", None),
            P(None, "src"),
            P(),
            P(),
            P(),
        ),
        out_specs=P(("tile", "src"), None),
        check_vma=False,
    )
```

```python
import math

import jax
import jax.numpy as jnp
from jax import lax
from jax.sharding import PartitionSpec as P

GRID = 16
SUB = 8
W = 32
REG = 64
PIX = 64
SRC_DEV = 4
PATCH = 256
ORD = 128
f32 = jnp.float32
bf16 = jnp.bfloat16


def split_bf16(x):
    hi = lax.reduce_precision(x, exponent_bits=8, mantissa_bits=7)
    lo = x - hi
    return hi.astype(bf16), lo.astype(bf16)


def phase_tables():
    turn = 2.0 * math.pi / PIX
    v = jnp.arange(ORD, dtype=jnp.int32)
    y = jnp.arange(PIX, dtype=jnp.int32)
    ang = jnp.mod(v[:, None] * y[None, :], PIX).astype(f32) * turn
    cv, sv = jnp.cos(ang), jnp.sin(ang)
    t1 = jnp.stack([jnp.concatenate([cv, sv], 1), jnp.concatenate([-sv, cv], 1)], 0)
    i = jnp.arange(W, dtype=jnp.int32)
    x = jnp.arange(PIX, dtype=jnp.int32)
    ang2 = jnp.mod(x[:, None] * i[None, :], PIX).astype(f32) * turn
    ca, sa = jnp.cos(ang2), jnp.sin(ang2)
    t2 = jnp.stack([jnp.stack([ca, -sa], 1), jnp.stack([sa, ca], 1)], 0)
    return t1, t2


def imaging(spec, source_index, source_cutoff, source_weight):
    T = spec.shape[0]
    S = source_index.shape[0]
    x0 = jnp.clip(source_index[:, 0], 0, ORD - W)
    y0 = jnp.clip(source_index[:, 1], 0, ORD - W)
    rows = x0[:, None] + jnp.arange(W, dtype=jnp.int32)[None, :]
    pick = (rows[:, :, None] == jnp.arange(ORD, dtype=jnp.int32)[None, None, :]).astype(bf16)
    spec_rows = spec.reshape(T, 6, 2, ORD, ORD)
    strips = jnp.einsum("siu,tkpuv->sitkpv", pick, spec_rows, preferred_element_type=f32).astype(bf16)
    i = jnp.arange(W, dtype=jnp.int32)
    j = jnp.arange(ORD, dtype=jnp.int32)[None, :] - y0[:, None]
    dist = (i[None, :, None] - W // 2) ** 2 + (j[:, None, :] - W // 2) ** 2
    keep = (dist <= (source_cutoff * source_cutoff)[:, None, None]) & (j[:, None, :] >= 0) & (j[:, None, :] < W)
    masked = jnp.where(keep[:, :, None, None, None, :], strips, jnp.zeros((), bf16))
    t1, t2 = phase_tables()
    t1h, t1l = split_bf16(t1)
    t1s = jnp.concatenate([t1h, t1l], -1)
    out1 = jnp.einsum("sitkpv,pvn->sitkn", masked, t1s, preferred_element_type=f32)
    half = out1[..., : 2 * PIX] + out1[..., 2 * PIX:]
    half = half.reshape(S, W, T, 6, 2, PIX)
    hh, hl = split_bf16(half)
    hcat = jnp.concatenate([hh, hl, hh], 4)
    t2h, t2l = split_bf16(t2)
    t2cat = jnp.concatenate([t2h, t2h, t2l], 2)
    field = jnp.einsum("cxqi,sitkqy->tskcxy", t2cat, hcat, preferred_element_type=f32)
    power = jnp.sum(field * field * source_weight[None, :, None, None, None, None], axis=(1, 2, 3))
    return power.reshape(T, PIX * PIX) * (1.0 / (6.0 * W * W * S))


def local(
    tile_tokens,
    norm_gain,
    up_weight,
    down_weight,
    head_weight,
    source_index,
    source_cutoff,
    source_weight,
):
    token_count, d_model = tile_tokens.shape
    n_tile = lax.axis_size("tile")
    n_src = lax.axis_size("src")
    me = lax.axis_index("src")
    half = me % 2
    up_rows, ff = up_weight.shape
    down_rows = down_weight.shape[0]
    up_half, down_half = up_rows // 2, down_rows // 2
    depth = max(up_half, down_half)
    width = max(ff, d_model)
    up_part = lax.dynamic_slice_in_dim(up_weight, half * up_half, up_half, 0)
    down_part = lax.dynamic_slice_in_dim(down_weight, half * down_half, down_half, 0)
    packed = jnp.stack(
        [
            jnp.pad(up_part, ((0, depth - up_half), (0, width - ff))),
            jnp.pad(down_part, ((0, depth - down_half), (0, width - d_model))),
        ],
        0,
    )
    gathered = lax.all_gather(packed, "tile", axis=1, tiled=False)
    sibling = lax.ppermute(gathered, "src", [(s, s ^ 1) for s in range(n_src)])
    head_parts = [head_weight] + [
        lax.ppermute(head_weight, "src", [(s, s ^ k) for s in range(n_src)]) for k in range(1, n_src)
    ]

    residual = tile_tokens.astype(jnp.float32)
    mean_square = jnp.mean(residual * residual, axis=1, keepdims=True)
    normed = (residual * lax.rsqrt(mean_square + 1e-05) * norm_gain).astype(jnp.bfloat16)

    def halves(x, rows):
        view = x.reshape(x.shape[0], n_tile, 2, rows // 2)
        pad = ((0, 0), (0, 0), (0, depth - rows // 2))
        mine = jnp.pad(lax.dynamic_index_in_dim(view, half, 2, keepdims=False), pad)
        other = jnp.pad(lax.dynamic_index_in_dim(view, 1 - half, 2, keepdims=False), pad)
        return mine.reshape(x.shape[0], -1), other.reshape(x.shape[0], -1)

    def weights(g):
        return g[0].reshape(n_tile * depth, width), g[1].reshape(n_tile * depth, width)

    up_mine, down_mine = weights(gathered)
    up_other, down_other = weights(sibling)
    normed_mine, normed_other = halves(normed, up_rows)
    pre_act = jnp.dot(normed_mine, up_mine, preferred_element_type=jnp.float32) + jnp.dot(
        normed_other, up_other, preferred_element_type=jnp.float32
    )
    hidden = jax.nn.gelu(pre_act[:, :ff]).astype(jnp.bfloat16)
    hidden_mine, hidden_other = halves(hidden, down_rows)
    branch_out = jnp.dot(hidden_mine, down_mine, preferred_element_type=jnp.float32) + jnp.dot(
        hidden_other, down_other, preferred_element_type=jnp.float32
    )
    branch_out = branch_out[:, :d_model]
    mixed = (residual + branch_out).astype(jnp.bfloat16)
    parts = jnp.stack(head_parts, 0)
    coeff_parts = jnp.einsum("tk,pkc->ptc", mixed, parts, preferred_element_type=jnp.float32).astype(
        jnp.bfloat16
    )
    order = me ^ jnp.arange(n_src, dtype=jnp.int32)
    coeffs = jnp.take(coeff_parts, order, axis=0).transpose(1, 0, 2).reshape(token_count, -1)
    tile_count = token_count // PATCH
    spectra = (
        coeffs.reshape(tile_count, GRID, GRID, 12, SUB, SUB)
        .transpose(0, 3, 1, 4, 2, 5)
        .reshape(tile_count, 12, ORD, ORD)
    )
    return imaging(spectra, source_index, source_cutoff, source_weight)


def solution(mesh):
    return jax.shard_map(
        local,
        mesh=mesh,
        in_specs=(
            P(("tile", "src"), None),
            P(),
            P("tile", None),
            P("tile", None),
            P(None, "src"),
            P(),
            P(),
            P(),
        ),
        out_specs=P(("tile", "src"), None),
        check_vma=False,
    )
```

```python
import math

import jax
import jax.numpy as jnp
from jax import lax
from jax.sharding import PartitionSpec as P

GRID = 16
SUB = 8
W = 32
REG = 64
PIX = 64
SRC_DEV = 4
PATCH = 256
ORD = 128
f32 = jnp.float32
bf16 = jnp.bfloat16


def split_bf16(x):
    hi = lax.reduce_precision(x, exponent_bits=8, mantissa_bits=7)
    lo = x - hi
    return hi.astype(bf16), lo.astype(bf16)


def phase_tables():
    turn = 2.0 * math.pi / PIX
    v = jnp.arange(ORD, dtype=jnp.int32)
    y = jnp.arange(PIX, dtype=jnp.int32)
    ang = jnp.mod(v[:, None] * y[None, :], PIX).astype(f32) * turn
    cv, sv = jnp.cos(ang), jnp.sin(ang)
    t1 = jnp.stack([jnp.concatenate([cv, sv], 1), jnp.concatenate([-sv, cv], 1)], 0)
    i = jnp.arange(W, dtype=jnp.int32)
    x = jnp.arange(PIX, dtype=jnp.int32)
    ang2 = jnp.mod(x[:, None] * i[None, :], PIX).astype(f32) * turn
    ca, sa = jnp.cos(ang2), jnp.sin(ang2)
    t2 = jnp.stack([jnp.stack([ca, -sa], 1), jnp.stack([sa, ca], 1)], 0)
    return t1, t2


def imaging(spec, source_index, source_cutoff, source_weight):
    T = spec.shape[0]
    S = source_index.shape[0]
    x0 = jnp.clip(source_index[:, 0], 0, ORD - W)
    y0 = jnp.clip(source_index[:, 1], 0, ORD - W)
    rows = x0[:, None] + jnp.arange(W, dtype=jnp.int32)[None, :]
    pick = (rows[:, :, None] == jnp.arange(ORD, dtype=jnp.int32)[None, None, :]).astype(bf16)
    spec_rows = spec.reshape(T, 6, 2, ORD, ORD)
    strips = jnp.einsum("siu,tkpuv->sitkpv", pick, spec_rows, preferred_element_type=f32).astype(bf16)
    i = jnp.arange(W, dtype=jnp.int32)
    j = jnp.arange(ORD, dtype=jnp.int32)[None, :] - y0[:, None]
    dist = (i[None, :, None] - W // 2) ** 2 + (j[:, None, :] - W // 2) ** 2
    keep = (dist <= (source_cutoff * source_cutoff)[:, None, None]) & (j[:, None, :] >= 0) & (j[:, None, :] < W)
    masked = jnp.where(keep[:, :, None, None, None, :], strips, jnp.zeros((), bf16))
    t1, t2 = phase_tables()
    t1h, t1l = split_bf16(t1)
    t1s = jnp.concatenate([t1h, t1l], -1)
    out1 = jnp.einsum("sitkpv,pvn->sitkn", masked, t1s, preferred_element_type=f32)
    half = out1[..., : 2 * PIX] + out1[..., 2 * PIX:]
    half = half.reshape(S, W, T, 6, 2, PIX)
    hh, hl = split_bf16(half)
    hcat = jnp.concatenate([hh, hl, hh], 4)
    t2h, t2l = split_bf16(t2)
    t2cat = jnp.concatenate([t2h, t2h, t2l], 2)
    field = jnp.einsum("cxqi,sitkqy->tskcxy", t2cat, hcat, preferred_element_type=f32)
    power = jnp.sum(field * field * source_weight[None, :, None, None, None, None], axis=(1, 2, 3))
    return power.reshape(T, PIX * PIX) * (1.0 / (6.0 * W * W * S))


def local(
    tile_tokens,
    norm_gain,
    up_weight,
    down_weight,
    head_weight,
    source_index,
    source_cutoff,
    source_weight,
):
    token_count, d_model = tile_tokens.shape
    n_tile = lax.axis_size("tile")
    n_src = lax.axis_size("src")
    me = lax.axis_index("src")
    half = me % 2
    up_rows, ff = up_weight.shape
    down_rows = down_weight.shape[0]
    up_half, down_half = up_rows // 2, down_rows // 2
    depth = -(-(up_half + down_half) // 16) * 16
    width = max(ff, d_model)
    up_part = lax.dynamic_slice_in_dim(up_weight, half * up_half, up_half, 0)
    down_part = lax.dynamic_slice_in_dim(down_weight, half * down_half, down_half, 0)
    packed = jnp.concatenate(
        [
            jnp.pad(up_part, ((0, 0), (0, width - ff))),
            jnp.pad(down_part, ((0, depth - up_half - down_half), (0, width - d_model))),
        ],
        0,
    )
    gathered = lax.all_gather(packed, "tile", axis=0, tiled=True)
    sibling = lax.ppermute(gathered, "src", [(s, s ^ 1) for s in range(n_src)])
    head_parts = [head_weight] + [
        lax.ppermute(head_weight, "src", [(s, s ^ k) for s in range(n_src)]) for k in range(1, n_src)
    ]

    residual = tile_tokens.astype(jnp.float32)
    mean_square = jnp.mean(residual * residual, axis=1, keepdims=True)
    normed = (residual * lax.rsqrt(mean_square + 1e-05) * norm_gain).astype(jnp.bfloat16)

    def spread(x, rows, start):
        view = x.reshape(x.shape[0], n_tile, 2, rows // 2)
        pad = ((0, 0), (0, 0), (start, depth - start - rows // 2))
        mine = jnp.pad(lax.dynamic_index_in_dim(view, half, 2, keepdims=False), pad)
        other = jnp.pad(lax.dynamic_index_in_dim(view, 1 - half, 2, keepdims=False), pad)
        return mine.reshape(x.shape[0], -1), other.reshape(x.shape[0], -1)

    normed_mine, normed_other = spread(normed, up_rows, 0)
    pre_act = jnp.dot(normed_mine, gathered, preferred_element_type=jnp.float32) + jnp.dot(
        normed_other, sibling, preferred_element_type=jnp.float32
    )
    hidden = jax.nn.gelu(pre_act[:, :ff]).astype(jnp.bfloat16)
    hidden_mine, hidden_other = spread(hidden, down_rows, up_half)
    branch_out = jnp.dot(hidden_mine, gathered, preferred_element_type=jnp.float32) + jnp.dot(
        hidden_other, sibling, preferred_element_type=jnp.float32
    )
    branch_out = branch_out[:, :d_model]
    mixed = (residual + branch_out).astype(jnp.bfloat16)
    parts = jnp.stack(head_parts, 0)
    coeff_parts = jnp.einsum("tk,pkc->ptc", mixed, parts, preferred_element_type=jnp.float32).astype(
        jnp.bfloat16
    )
    order = me ^ jnp.arange(n_src, dtype=jnp.int32)
    coeffs = jnp.take(coeff_parts, order, axis=0).transpose(1, 0, 2).reshape(token_count, -1)
    tile_count = token_count // PATCH
    spectra = (
        coeffs.reshape(tile_count, GRID, GRID, 12, SUB, SUB)
        .transpose(0, 3, 1, 4, 2, 5)
        .reshape(tile_count, 12, ORD, ORD)
    )
    return imaging(spectra, source_index, source_cutoff, source_weight)


def solution(mesh):
    return jax.shard_map(
        local,
        mesh=mesh,
        in_specs=(
            P(("tile", "src"), None),
            P(),
            P("tile", None),
            P("tile", None),
            P(None, "src"),
            P(),
            P(),
            P(),
        ),
        out_specs=P(("tile", "src"), None),
        check_vma=False,
    )
```

```python
import math

import jax
import jax.numpy as jnp
from jax import lax
from jax.sharding import PartitionSpec as P

GRID = 16
SUB = 8
W = 32
REG = 64
PIX = 64
SRC_DEV = 4
PATCH = 256
ORD = 128
f32 = jnp.float32
bf16 = jnp.bfloat16


def split_bf16(x):
    hi = lax.reduce_precision(x, exponent_bits=8, mantissa_bits=7)
    lo = x - hi
    return hi.astype(bf16), lo.astype(bf16)


def phase_tables():
    turn = 2.0 * math.pi / PIX
    v = jnp.arange(ORD, dtype=jnp.int32)
    y = jnp.arange(PIX, dtype=jnp.int32)
    ang = jnp.mod(v[:, None] * y[None, :], PIX).astype(f32) * turn
    cv, sv = jnp.cos(ang), jnp.sin(ang)
    t1 = jnp.stack([jnp.concatenate([cv, sv], 1), jnp.concatenate([-sv, cv], 1)], 0)
    i = jnp.arange(W, dtype=jnp.int32)
    x = jnp.arange(PIX, dtype=jnp.int32)
    ang2 = jnp.mod(x[:, None] * i[None, :], PIX).astype(f32) * turn
    ca, sa = jnp.cos(ang2), jnp.sin(ang2)
    t2 = jnp.stack([jnp.stack([ca, -sa], 1), jnp.stack([sa, ca], 1)], 0)
    return t1, t2


def imaging(spec, source_index, source_cutoff, source_weight):
    T = spec.shape[0]
    S = source_index.shape[0]
    x0 = jnp.clip(source_index[:, 0], 0, ORD - W)
    y0 = jnp.clip(source_index[:, 1], 0, ORD - W)
    rows = x0[:, None] + jnp.arange(W, dtype=jnp.int32)[None, :]
    pick = (rows[:, :, None] == jnp.arange(ORD, dtype=jnp.int32)[None, None, :]).astype(bf16)
    spec_rows = spec.reshape(T, 6, 2, ORD, ORD)
    strips = jnp.einsum("siu,tkpuv->sitkpv", pick, spec_rows, preferred_element_type=f32).astype(bf16)
    i = jnp.arange(W, dtype=jnp.int32)
    j = jnp.arange(ORD, dtype=jnp.int32)[None, :] - y0[:, None]
    dist = (i[None, :, None] - W // 2) ** 2 + (j[:, None, :] - W // 2) ** 2
    keep = (dist <= (source_cutoff * source_cutoff)[:, None, None]) & (j[:, None, :] >= 0) & (j[:, None, :] < W)
    masked = jnp.where(keep[:, :, None, None, None, :], strips, jnp.zeros((), bf16))
    t1, t2 = phase_tables()
    half = jnp.einsum("sitkpv,pvn->sitkn", masked.astype(f32), t1, precision=lax.Precision.HIGH)
    half = half.reshape(S, W, T, 6, 2, PIX)
    field = jnp.einsum("cxqi,sitkqy->tskcxy", t2, half, precision=lax.Precision.HIGH)
    power = jnp.sum(field * field * source_weight[None, :, None, None, None, None], axis=(1, 2, 3))
    return power.reshape(T, PIX * PIX) * (1.0 / (6.0 * W * W * S))


def local(
    tile_tokens,
    norm_gain,
    up_weight,
    down_weight,
    head_weight,
    source_index,
    source_cutoff,
    source_weight,
):
    token_count, d_model = tile_tokens.shape
    n_tile = lax.axis_size("tile")
    n_src = lax.axis_size("src")
    me = lax.axis_index("src")
    half = me % 2
    up_rows, ff = up_weight.shape
    down_rows = down_weight.shape[0]
    up_half, down_half = up_rows // 2, down_rows // 2
    depth = -(-(up_half + down_half) // 16) * 16
    width = max(ff, d_model)
    up_part = lax.dynamic_slice_in_dim(up_weight, half * up_half, up_half, 0)
    down_part = lax.dynamic_slice_in_dim(down_weight, half * down_half, down_half, 0)
    packed = jnp.concatenate(
        [
            jnp.pad(up_part, ((0, 0), (0, width - ff))),
            jnp.pad(down_part, ((0, depth - up_half - down_half), (0, width - d_model))),
        ],
        0,
    )
    gathered = lax.all_gather(packed, "tile", axis=0, tiled=True)
    sibling = lax.ppermute(gathered, "src", [(s, s ^ 1) for s in range(n_src)])
    head_parts = [head_weight] + [
        lax.ppermute(head_weight, "src", [(s, s ^ k) for s in range(n_src)]) for k in range(1, n_src)
    ]

    residual = tile_tokens.astype(jnp.float32)
    mean_square = jnp.mean(residual * residual, axis=1, keepdims=True)
    normed = (residual * lax.rsqrt(mean_square + 1e-05) * norm_gain).astype(jnp.bfloat16)

    def spread(x, rows, start):
        view = x.reshape(x.shape[0], n_tile, 2, rows // 2)
        pad = ((0, 0), (0, 0), (start, depth - start - rows // 2))
        mine = jnp.pad(lax.dynamic_index_in_dim(view, half, 2, keepdims=False), pad)
        other = jnp.pad(lax.dynamic_index_in_dim(view, 1 - half, 2, keepdims=False), pad)
        return mine.reshape(x.shape[0], -1), other.reshape(x.shape[0], -1)

    normed_mine, normed_other = spread(normed, up_rows, 0)
    pre_act = jnp.dot(normed_mine, gathered, preferred_element_type=jnp.float32) + jnp.dot(
        normed_other, sibling, preferred_element_type=jnp.float32
    )
    hidden = jax.nn.gelu(pre_act[:, :ff]).astype(jnp.bfloat16)
    hidden_mine, hidden_other = spread(hidden, down_rows, up_half)
    branch_out = jnp.dot(hidden_mine, gathered, preferred_element_type=jnp.float32) + jnp.dot(
        hidden_other, sibling, preferred_element_type=jnp.float32
    )
    branch_out = branch_out[:, :d_model]
    mixed = (residual + branch_out).astype(jnp.bfloat16)
    parts = jnp.stack(head_parts, 0)
    coeff_parts = jnp.einsum("tk,pkc->ptc", mixed, parts, preferred_element_type=jnp.float32).astype(
        jnp.bfloat16
    )
    order = me ^ jnp.arange(n_src, dtype=jnp.int32)
    coeffs = jnp.take(coeff_parts, order, axis=0).transpose(1, 0, 2).reshape(token_count, -1)
    tile_count = token_count // PATCH
    spectra = (
        coeffs.reshape(tile_count, GRID, GRID, 12, SUB, SUB)
        .transpose(0, 3, 1, 4, 2, 5)
        .reshape(tile_count, 12, ORD, ORD)
    )
    return imaging(spectra, source_index, source_cutoff, source_weight)


def solution(mesh):
    return jax.shard_map(
        local,
        mesh=mesh,
        in_specs=(
            P(("tile", "src"), None),
            P(),
            P("tile", None),
            P("tile", None),
            P(None, "src"),
            P(),
            P(),
            P(),
        ),
        out_specs=P(("tile", "src"), None),
        check_vma=False,
    )
```

```python
import functools
import math

import jax
import jax.numpy as jnp
from jax import lax
from jax.experimental import pallas as pl
from jax.experimental.pallas import tpu as pltpu
from jax.sharding import PartitionSpec as P

GRID = 16
SUB = 8
W = 32
REG = 64
PIX = 64
SRC_DEV = 4
PATCH = 256
ORD = 128
f32 = jnp.float32
bf16 = jnp.bfloat16


def split_bf16(x):
    hi = lax.reduce_precision(x, exponent_bits=8, mantissa_bits=7)
    lo = x - hi
    return hi.astype(bf16), lo.astype(bf16)


def phase_tables():
    turn = 2.0 * math.pi / PIX
    v = jnp.arange(ORD, dtype=jnp.int32)
    y = jnp.arange(PIX, dtype=jnp.int32)
    ang = jnp.mod(v[:, None] * y[None, :], PIX).astype(f32) * turn
    cv, sv = jnp.cos(ang), jnp.sin(ang)
    t1 = jnp.concatenate([jnp.concatenate([cv, sv], 1), jnp.concatenate([-sv, cv], 1)], 0)
    i = jnp.arange(W, dtype=jnp.int32)
    x = jnp.arange(PIX, dtype=jnp.int32)
    ang2 = jnp.mod(x[:, None] * i[None, :], PIX).astype(f32) * turn
    t2 = jnp.concatenate([jnp.cos(ang2), jnp.sin(ang2)], 0)
    return t1, t2


def power_kernel(w_ref, wm_ref, t1_ref, t2_ref, out_ref, rcat, *, sb):
    step = pl.program_id(0)
    blocks = sb * 6
    x = wm_ref[...].reshape(blocks * W, 2 * ORD)
    y = jnp.dot(x, t1_ref[...], preferred_element_type=f32)
    h = y[:, : 2 * PIX] + y[:, 2 * PIX:]
    hh = h.astype(bf16)
    hl = (h - hh.astype(f32)).astype(bf16)
    rcat[3 * W:, :] = jnp.zeros((W, blocks * 2 * PIX), bf16)
    for n in range(blocks):
        cols = slice(n * 2 * PIX, (n + 1) * 2 * PIX)
        rows = slice(n * W, (n + 1) * W)
        rcat[0:W, cols] = hh[rows, :]
        rcat[W:2 * W, cols] = hl[rows, :]
        rcat[2 * W:3 * W, cols] = hh[rows, :]
    q = jnp.dot(t2_ref[...], rcat[...], preferred_element_type=f32)
    acc = jnp.zeros((PIX, 2 * PIX), f32)
    for j in range(sb):
        part = jnp.zeros((PIX, 2 * PIX), f32)
        for k in range(6):
            n = j * 6 + k
            blk = q[:, n * 2 * PIX:(n + 1) * 2 * PIX]
            rolled = pltpu.roll(blk, PIX, 1)
            er = blk[:PIX] - rolled[PIX:]
            ei = blk[PIX:] + rolled[:PIX]
            part = part + er * er + ei * ei
        acc = acc + w_ref[step * sb + j] * part

    @pl.when(step == 0)
    def _():
        out_ref[...] = jnp.zeros_like(out_ref)

    out_ref[...] += acc


def imaging(spec, source_index, source_cutoff, source_weight, sb=8):
    T = spec.shape[0]
    S = source_index.shape[0]
    x0 = jnp.clip(source_index[:, 0], 0, ORD - W)
    y0 = jnp.clip(source_index[:, 1], 0, ORD - W)
    rows = x0[:, None] + jnp.arange(W, dtype=jnp.int32)[None, :]
    pick = (rows[:, :, None] == jnp.arange(ORD, dtype=jnp.int32)[None, None, :]).astype(bf16)
    spec_rows = spec.reshape(T, 6, 2, ORD, ORD)
    strips = jnp.einsum("siu,tkpuv->tskipv", pick, spec_rows, preferred_element_type=f32)
    i = jnp.arange(W, dtype=jnp.int32)
    j = jnp.arange(ORD, dtype=jnp.int32)[None, :] - y0[:, None]
    dist = (i[None, :, None] - W // 2) ** 2 + (j[:, None, :] - W // 2) ** 2
    keep = (dist <= (source_cutoff * source_cutoff)[:, None, None]) & (j[:, None, :] >= 0) & (j[:, None, :] < W)
    masked = jnp.where(keep[None, :, None, :, None, :], strips, 0.0).astype(bf16)
    masked = masked.reshape(T, S, 6, W, 2 * ORD)
    t1, t2 = phase_tables()
    t1h, t1l = split_bf16(t1)
    t1s = jnp.concatenate([t1h, t1l], 1)
    t2h, t2l = split_bf16(t2)
    t2c = jnp.concatenate([t2h, t2h, t2l, jnp.zeros((2 * PIX, W), bf16)], 1)
    call = pl.pallas_call(
        functools.partial(power_kernel, sb=sb),
        out_shape=jax.ShapeDtypeStruct((PIX, 2 * PIX), f32),
        grid=(S // sb,),
        in_specs=[
            pl.BlockSpec(memory_space=pltpu.SMEM),
            pl.BlockSpec((sb, 6, W, 2 * ORD), lambda s: (s, 0, 0, 0)),
            pl.BlockSpec((2 * ORD, 4 * PIX), lambda s: (0, 0)),
            pl.BlockSpec((2 * PIX, 4 * W), lambda s: (0, 0)),
        ],
        out_specs=pl.BlockSpec((PIX, 2 * PIX), lambda s: (0, 0)),
        scratch_shapes=[pltpu.VMEM((4 * W, sb * 6 * 2 * PIX), bf16)],
        compiler_params=pltpu.CompilerParams(dimension_semantics=("arbitrary",)),
    )
    outs = [call(source_weight.astype(f32), masked[t], t1s, t2c)[:, :PIX] for t in range(T)]
    power = jnp.stack(outs, 0)
    return power.reshape(T, PIX * PIX) * (1.0 / (6.0 * W * W * S))


def local(
    tile_tokens,
    norm_gain,
    up_weight,
    down_weight,
    head_weight,
    source_index,
    source_cutoff,
    source_weight,
):
    token_count, d_model = tile_tokens.shape
    n_tile = lax.axis_size("tile")
    n_src = lax.axis_size("src")
    me = lax.axis_index("src")
    half = me % 2
    up_rows, ff = up_weight.shape
    down_rows = down_weight.shape[0]
    up_half, down_half = up_rows // 2, down_rows // 2
    depth = -(-(up_half + down_half) // 16) * 16
    width = max(ff, d_model)
    up_part = lax.dynamic_slice_in_dim(up_weight, half * up_half, up_half, 0)
    down_part = lax.dynamic_slice_in_dim(down_weight, half * down_half, down_half, 0)
    packed = jnp.concatenate(
        [
            jnp.pad(up_part, ((0, 0), (0, width - ff))),
            jnp.pad(down_part, ((0, depth - up_half - down_half), (0, width - d_model))),
        ],
        0,
    )
    gathered = lax.all_gather(packed, "tile", axis=0, tiled=True)
    sibling = lax.ppermute(gathered, "src", [(s, s ^ 1) for s in range(n_src)])
    head_parts = [head_weight] + [
        lax.ppermute(head_weight, "src", [(s, s ^ k) for s in range(n_src)]) for k in range(1, n_src)
    ]

    residual = tile_tokens.astype(jnp.float32)
    mean_square = jnp.mean(residual * residual, axis=1, keepdims=True)
    normed = (residual * lax.rsqrt(mean_square + 1e-05) * norm_gain).astype(jnp.bfloat16)

    def spread(x, rows, start):
        view = x.reshape(x.shape[0], n_tile, 2, rows // 2)
        pad = ((0, 0), (0, 0), (start, depth - start - rows // 2))
        mine = jnp.pad(lax.dynamic_index_in_dim(view, half, 2, keepdims=False), pad)
        other = jnp.pad(lax.dynamic_index_in_dim(view, 1 - half, 2, keepdims=False), pad)
        return mine.reshape(x.shape[0], -1), other.reshape(x.shape[0], -1)

    normed_mine, normed_other = spread(normed, up_rows, 0)
    pre_act = jnp.dot(normed_mine, gathered, preferred_element_type=jnp.float32) + jnp.dot(
        normed_other, sibling, preferred_element_type=jnp.float32
    )
    hidden = jax.nn.gelu(pre_act[:, :ff]).astype(jnp.bfloat16)
    hidden_mine, hidden_other = spread(hidden, down_rows, up_half)
    branch_out = jnp.dot(hidden_mine, gathered, preferred_element_type=jnp.float32) + jnp.dot(
        hidden_other, sibling, preferred_element_type=jnp.float32
    )
    branch_out = branch_out[:, :d_model]
    mixed = (residual + branch_out).astype(jnp.bfloat16)
    parts = jnp.stack(head_parts, 0)
    coeff_parts = jnp.einsum("tk,pkc->ptc", mixed, parts, preferred_element_type=jnp.float32).astype(
        jnp.bfloat16
    )
    order = me ^ jnp.arange(n_src, dtype=jnp.int32)
    coeffs = jnp.take(coeff_parts, order, axis=0).transpose(1, 0, 2).reshape(token_count, -1)
    tile_count = token_count // PATCH
    spectra = (
        coeffs.reshape(tile_count, GRID, GRID, 12, SUB, SUB)
        .transpose(0, 3, 1, 4, 2, 5)
        .reshape(tile_count, 12, ORD, ORD)
    )
    return imaging(spectra, source_index, source_cutoff, source_weight)


def solution(mesh):
    return jax.shard_map(
        local,
        mesh=mesh,
        in_specs=(
            P(("tile", "src"), None),
            P(),
            P("tile", None),
            P("tile", None),
            P(None, "src"),
            P(),
            P(),
            P(),
        ),
        out_specs=P(("tile", "src"), None),
        check_vma=False,
    )
```

```python
import functools
import math

import jax
import jax.numpy as jnp
from jax import lax
from jax.experimental import pallas as pl
from jax.experimental.pallas import tpu as pltpu
from jax.sharding import PartitionSpec as P

GRID = 16
SUB = 8
W = 32
REG = 64
PIX = 64
SRC_DEV = 4
PATCH = 256
ORD = 128
f32 = jnp.float32
bf16 = jnp.bfloat16


def split_bf16(x):
    hi = lax.reduce_precision(x, exponent_bits=8, mantissa_bits=7)
    lo = x - hi
    return hi.astype(bf16), lo.astype(bf16)


def phase_tables():
    turn = 2.0 * math.pi / PIX
    v = jnp.arange(ORD, dtype=jnp.int32)
    y = jnp.arange(PIX, dtype=jnp.int32)
    ang = jnp.mod(v[:, None] * y[None, :], PIX).astype(f32) * turn
    cv, sv = jnp.cos(ang), jnp.sin(ang)
    t1 = jnp.concatenate([jnp.concatenate([cv, sv], 1), jnp.concatenate([-sv, cv], 1)], 0)
    i = jnp.arange(W, dtype=jnp.int32)
    x = jnp.arange(PIX, dtype=jnp.int32)
    ang2 = jnp.mod(x[:, None] * i[None, :], PIX).astype(f32) * turn
    t2 = jnp.concatenate([jnp.cos(ang2), jnp.sin(ang2)], 0)
    return t1, t2


def power_kernel(w_ref, *refs, sb):
    wm_refs, (t1_ref, t2_ref, out_ref, rcat) = refs[:6], refs[6:]
    step = pl.program_id(0)
    rcat[3 * W:, :] = jnp.zeros((W, sb * 6 * 2 * PIX), bf16)
    for k in range(6):
        x = wm_refs[k][...].reshape(sb * W, 2 * ORD)
        y = jnp.dot(x, t1_ref[...], preferred_element_type=f32)
        h = y[:, : 2 * PIX] + y[:, 2 * PIX:]
        hh = h.astype(bf16)
        hl = (h - hh.astype(f32)).astype(bf16)
        for j in range(sb):
            n = k * sb + j
            cols = slice(n * 2 * PIX, (n + 1) * 2 * PIX)
            rows = slice(j * W, (j + 1) * W)
            rcat[0:W, cols] = hh[rows, :]
            rcat[W:2 * W, cols] = hl[rows, :]
            rcat[2 * W:3 * W, cols] = hh[rows, :]
    q = jnp.dot(t2_ref[...], rcat[...], preferred_element_type=f32)
    acc = jnp.zeros((PIX, 2 * PIX), f32)
    for j in range(sb):
        part = jnp.zeros((PIX, 2 * PIX), f32)
        for k in range(6):
            n = k * sb + j
            blk = q[:, n * 2 * PIX:(n + 1) * 2 * PIX]
            rolled = pltpu.roll(blk, PIX, 1)
            er = blk[:PIX] - rolled[PIX:]
            ei = blk[PIX:] + rolled[:PIX]
            part = part + er * er + ei * ei
        acc = acc + w_ref[step * sb + j] * part

    @pl.when(step == 0)
    def _():
        out_ref[...] = jnp.zeros_like(out_ref)

    out_ref[...] += acc


def imaging(spec, source_index, source_cutoff, source_weight, sb=8):
    T = spec.shape[0]
    S = source_index.shape[0]
    x0 = jnp.clip(source_index[:, 0], 0, ORD - W)
    y0 = jnp.clip(source_index[:, 1], 0, ORD - W)
    rows = x0[:, None] + jnp.arange(W, dtype=jnp.int32)[None, :]
    pick = (rows[:, :, None] == jnp.arange(ORD, dtype=jnp.int32)[None, None, :]).astype(bf16)
    spec_rows = spec.reshape(T, 6, 2, ORD, ORD).transpose(0, 1, 3, 2, 4).reshape(T, 6, ORD, 2 * ORD)
    i = jnp.arange(W, dtype=jnp.int32)
    j = jnp.arange(ORD, dtype=jnp.int32)[None, :] - y0[:, None]
    dist = (i[None, :, None] - W // 2) ** 2 + (j[:, None, :] - W // 2) ** 2
    keep = (dist <= (source_cutoff * source_cutoff)[:, None, None]) & (j[:, None, :] >= 0) & (j[:, None, :] < W)
    keep = jnp.concatenate([keep, keep], 2)
    t1, t2 = phase_tables()
    t1h, t1l = split_bf16(t1)
    t1s = jnp.concatenate([t1h, t1l], 1)
    t2h, t2l = split_bf16(t2)
    t2c = jnp.concatenate([t2h, t2h, t2l, jnp.zeros((2 * PIX, W), bf16)], 1)
    block = pl.BlockSpec((sb, W, 2 * ORD), lambda s: (s, 0, 0))
    call = pl.pallas_call(
        functools.partial(power_kernel, sb=sb),
        out_shape=jax.ShapeDtypeStruct((PIX, 2 * PIX), f32),
        grid=(S // sb,),
        in_specs=[pl.BlockSpec(memory_space=pltpu.SMEM)]
        + [block] * 6
        + [
            pl.BlockSpec((2 * ORD, 4 * PIX), lambda s: (0, 0)),
            pl.BlockSpec((2 * PIX, 4 * W), lambda s: (0, 0)),
        ],
        out_specs=pl.BlockSpec((PIX, 2 * PIX), lambda s: (0, 0)),
        scratch_shapes=[pltpu.VMEM((4 * W, sb * 6 * 2 * PIX), bf16)],
        compiler_params=pltpu.CompilerParams(dimension_semantics=("arbitrary",)),
    )
    outs = []
    for t in range(T):
        parts = []
        for k in range(6):
            strips = jnp.einsum("siu,un->sin", pick, spec_rows[t, k], preferred_element_type=f32)
            parts.append(jnp.where(keep, strips, 0.0).astype(bf16))
        outs.append(call(source_weight.astype(f32), *parts, t1s, t2c)[:, :PIX])
    power = jnp.stack(outs, 0)
    return power.reshape(T, PIX * PIX) * (1.0 / (6.0 * W * W * S))


def local(
    tile_tokens,
    norm_gain,
    up_weight,
    down_weight,
    head_weight,
    source_index,
    source_cutoff,
    source_weight,
):
    token_count, d_model = tile_tokens.shape
    n_tile = lax.axis_size("tile")
    n_src = lax.axis_size("src")
    me = lax.axis_index("src")
    half = me % 2
    up_rows, ff = up_weight.shape
    down_rows = down_weight.shape[0]
    up_half, down_half = up_rows // 2, down_rows // 2
    depth = -(-(up_half + down_half) // 16) * 16
    width = max(ff, d_model)
    up_part = lax.dynamic_slice_in_dim(up_weight, half * up_half, up_half, 0)
    down_part = lax.dynamic_slice_in_dim(down_weight, half * down_half, down_half, 0)
    packed = jnp.concatenate(
        [
            jnp.pad(up_part, ((0, 0), (0, width - ff))),
            jnp.pad(down_part, ((0, depth - up_half - down_half), (0, width - d_model))),
        ],
        0,
    )
    gathered = lax.all_gather(packed, "tile", axis=0, tiled=True)
    sibling = lax.ppermute(gathered, "src", [(s, s ^ 1) for s in range(n_src)])
    head_parts = [head_weight] + [
        lax.ppermute(head_weight, "src", [(s, s ^ k) for s in range(n_src)]) for k in range(1, n_src)
    ]

    residual = tile_tokens.astype(jnp.float32)
    mean_square = jnp.mean(residual * residual, axis=1, keepdims=True)
    normed = (residual * lax.rsqrt(mean_square + 1e-05) * norm_gain).astype(jnp.bfloat16)

    def spread(x, rows, start):
        view = x.reshape(x.shape[0], n_tile, 2, rows // 2)
        pad = ((0, 0), (0, 0), (start, depth - start - rows // 2))
        mine = jnp.pad(lax.dynamic_index_in_dim(view, half, 2, keepdims=False), pad)
        other = jnp.pad(lax.dynamic_index_in_dim(view, 1 - half, 2, keepdims=False), pad)
        return mine.reshape(x.shape[0], -1), other.reshape(x.shape[0], -1)

    normed_mine, normed_other = spread(normed, up_rows, 0)
    pre_act = jnp.dot(normed_mine, gathered, preferred_element_type=jnp.float32) + jnp.dot(
        normed_other, sibling, preferred_element_type=jnp.float32
    )
    hidden = jax.nn.gelu(pre_act[:, :ff]).astype(jnp.bfloat16)
    hidden_mine, hidden_other = spread(hidden, down_rows, up_half)
    branch_out = jnp.dot(hidden_mine, gathered, preferred_element_type=jnp.float32) + jnp.dot(
        hidden_other, sibling, preferred_element_type=jnp.float32
    )
    branch_out = branch_out[:, :d_model]
    mixed = (residual + branch_out).astype(jnp.bfloat16)
    parts = jnp.stack(head_parts, 0)
    coeff_parts = jnp.einsum("tk,pkc->ptc", mixed, parts, preferred_element_type=jnp.float32).astype(
        jnp.bfloat16
    )
    order = me ^ jnp.arange(n_src, dtype=jnp.int32)
    coeffs = jnp.take(coeff_parts, order, axis=0).transpose(1, 0, 2).reshape(token_count, -1)
    tile_count = token_count // PATCH
    spectra = (
        coeffs.reshape(tile_count, GRID, GRID, 12, SUB, SUB)
        .transpose(0, 3, 1, 4, 2, 5)
        .reshape(tile_count, 12, ORD, ORD)
    )
    return imaging(spectra, source_index, source_cutoff, source_weight)


def solution(mesh):
    return jax.shard_map(
        local,
        mesh=mesh,
        in_specs=(
            P(("tile", "src"), None),
            P(),
            P("tile", None),
            P("tile", None),
            P(None, "src"),
            P(),
            P(),
            P(),
        ),
        out_specs=P(("tile", "src"), None),
        check_vma=False,
    )
```

```python
import functools
import math

import jax
import jax.numpy as jnp
from jax import lax
from jax.experimental import pallas as pl
from jax.experimental.pallas import tpu as pltpu
from jax.sharding import PartitionSpec as P

GRID = 16
SUB = 8
W = 32
REG = 64
PIX = 64
SRC_DEV = 4
PATCH = 256
ORD = 128
f32 = jnp.float32
bf16 = jnp.bfloat16


def split_bf16(x):
    hi = lax.reduce_precision(x, exponent_bits=8, mantissa_bits=7)
    lo = x - hi
    return hi.astype(bf16), lo.astype(bf16)


def phase_tables():
    turn = 2.0 * math.pi / PIX
    v = jnp.arange(ORD, dtype=jnp.int32)
    y = jnp.arange(PIX, dtype=jnp.int32)
    ang = jnp.mod(v[:, None] * y[None, :], PIX).astype(f32) * turn
    cv, sv = jnp.cos(ang), jnp.sin(ang)
    t1 = jnp.concatenate([jnp.concatenate([cv, sv], 1), jnp.concatenate([-sv, cv], 1)], 0)
    i = jnp.arange(W, dtype=jnp.int32)
    x = jnp.arange(PIX, dtype=jnp.int32)
    ang2 = jnp.mod(x[:, None] * i[None, :], PIX).astype(f32) * turn
    t2 = jnp.concatenate([jnp.cos(ang2), jnp.sin(ang2)], 0)
    return t1, t2


def power_kernel(w_ref, *refs, sb):
    wm_refs, (t1_ref, t2_ref, out_ref, rcat) = refs[:6], refs[6:]
    step = pl.program_id(0)
    rcat[3 * W:, :] = jnp.zeros((W, sb * 6 * 2 * PIX), bf16)
    for k in range(6):
        x = wm_refs[k][...].reshape(sb * W, 2 * ORD)
        y = jnp.dot(x, t1_ref[...], preferred_element_type=f32)
        h = y[:, : 2 * PIX] + y[:, 2 * PIX:]
        hh = h.astype(bf16)
        hl = (h - hh.astype(f32)).astype(bf16)
        for j in range(sb):
            n = k * sb + j
            cols = slice(n * 2 * PIX, (n + 1) * 2 * PIX)
            rows = slice(j * W, (j + 1) * W)
            rcat[0:W, cols] = hh[rows, :]
            rcat[W:2 * W, cols] = hl[rows, :]
            rcat[2 * W:3 * W, cols] = hh[rows, :]
    q = jnp.dot(t2_ref[...], rcat[...], preferred_element_type=f32)
    acc = jnp.zeros((PIX, 2 * PIX), f32)
    for j in range(sb):
        part = jnp.zeros((PIX, 2 * PIX), f32)
        for k in range(6):
            n = k * sb + j
            blk = q[:, n * 2 * PIX:(n + 1) * 2 * PIX]
            rolled = pltpu.roll(blk, PIX, 1)
            er = blk[:PIX] - rolled[PIX:]
            ei = blk[PIX:] + rolled[:PIX]
            part = part + er * er + ei * ei
        acc = acc + w_ref[step * sb + j] * part

    @pl.when(step == 0)
    def _():
        out_ref[...] = jnp.zeros_like(out_ref)

    out_ref[...] += acc


def imaging(spec_rows, source_index, source_cutoff, source_weight, sb=8):
    T = spec_rows.shape[0]
    S = source_index.shape[0]
    x0 = jnp.clip(source_index[:, 0], 0, ORD - W)
    y0 = jnp.clip(source_index[:, 1], 0, ORD - W)
    rows = x0[:, None] + jnp.arange(W, dtype=jnp.int32)[None, :]
    pick = (rows[:, :, None] == jnp.arange(ORD, dtype=jnp.int32)[None, None, :]).astype(bf16)
    i = jnp.arange(W, dtype=jnp.int32)
    j = jnp.arange(ORD, dtype=jnp.int32)[None, :] - y0[:, None]
    dist = (i[None, :, None] - W // 2) ** 2 + (j[:, None, :] - W // 2) ** 2
    keep = (dist <= (source_cutoff * source_cutoff)[:, None, None]) & (j[:, None, :] >= 0) & (j[:, None, :] < W)
    keep = jnp.tile(keep, (1, 1, 12))
    t1, t2 = phase_tables()
    t1h, t1l = split_bf16(t1)
    t1s = jnp.concatenate([t1h, t1l], 1)
    t2h, t2l = split_bf16(t2)
    t2c = jnp.concatenate([t2h, t2h, t2l, jnp.zeros((2 * PIX, W), bf16)], 1)
    blocks = [pl.BlockSpec((sb, W, 2 * ORD), functools.partial(lambda k, s: (s, 0, k), k)) for k in range(6)]
    call = pl.pallas_call(
        functools.partial(power_kernel, sb=sb),
        out_shape=jax.ShapeDtypeStruct((PIX, 2 * PIX), f32),
        grid=(S // sb,),
        in_specs=[pl.BlockSpec(memory_space=pltpu.SMEM)]
        + blocks
        + [
            pl.BlockSpec((2 * ORD, 4 * PIX), lambda s: (0, 0)),
            pl.BlockSpec((2 * PIX, 4 * W), lambda s: (0, 0)),
        ],
        out_specs=pl.BlockSpec((PIX, 2 * PIX), lambda s: (0, 0)),
        scratch_shapes=[pltpu.VMEM((4 * W, sb * 6 * 2 * PIX), bf16)],
        compiler_params=pltpu.CompilerParams(dimension_semantics=("arbitrary",)),
    )
    outs = []
    for t in range(T):
        strips = jnp.einsum("siu,un->sin", pick, spec_rows[t], preferred_element_type=f32)
        windows = jnp.where(keep, strips, 0.0).astype(bf16)
        outs.append(call(source_weight.astype(f32), *([windows] * 6), t1s, t2c)[:, :PIX])
    power = jnp.stack(outs, 0)
    return power.reshape(T, PIX * PIX) * (1.0 / (6.0 * W * W * S))


def local(
    tile_tokens,
    norm_gain,
    up_weight,
    down_weight,
    head_weight,
    source_index,
    source_cutoff,
    source_weight,
):
    token_count, d_model = tile_tokens.shape
    n_tile = lax.axis_size("tile")
    n_src = lax.axis_size("src")
    me = lax.axis_index("src")
    half = me % 2
    up_rows, ff = up_weight.shape
    down_rows = down_weight.shape[0]
    up_half, down_half = up_rows // 2, down_rows // 2
    depth = -(-(up_half + down_half) // 16) * 16
    width = max(ff, d_model)
    up_part = lax.dynamic_slice_in_dim(up_weight, half * up_half, up_half, 0)
    down_part = lax.dynamic_slice_in_dim(down_weight, half * down_half, down_half, 0)
    packed = jnp.concatenate(
        [
            jnp.pad(up_part, ((0, 0), (0, width - ff))),
            jnp.pad(down_part, ((0, depth - up_half - down_half), (0, width - d_model))),
        ],
        0,
    )
    gathered = lax.all_gather(packed, "tile", axis=0, tiled=True)
    sibling = lax.ppermute(gathered, "src", [(s, s ^ 1) for s in range(n_src)])
    head_parts = [head_weight] + [
        lax.ppermute(head_weight, "src", [(s, s ^ k) for s in range(n_src)]) for k in range(1, n_src)
    ]

    residual = tile_tokens.astype(jnp.float32)
    mean_square = jnp.mean(residual * residual, axis=1, keepdims=True)
    normed = (residual * lax.rsqrt(mean_square + 1e-05) * norm_gain).astype(jnp.bfloat16)

    def spread(x, rows, start):
        view = x.reshape(x.shape[0], n_tile, 2, rows // 2)
        pad = ((0, 0), (0, 0), (start, depth - start - rows // 2))
        mine = jnp.pad(lax.dynamic_index_in_dim(view, half, 2, keepdims=False), pad)
        other = jnp.pad(lax.dynamic_index_in_dim(view, 1 - half, 2, keepdims=False), pad)
        return mine.reshape(x.shape[0], -1), other.reshape(x.shape[0], -1)

    normed_mine, normed_other = spread(normed, up_rows, 0)
    pre_act = jnp.dot(normed_mine, gathered, preferred_element_type=jnp.float32) + jnp.dot(
        normed_other, sibling, preferred_element_type=jnp.float32
    )
    hidden = jax.nn.gelu(pre_act[:, :ff]).astype(jnp.bfloat16)
    hidden_mine, hidden_other = spread(hidden, down_rows, up_half)
    branch_out = jnp.dot(hidden_mine, gathered, preferred_element_type=jnp.float32) + jnp.dot(
        hidden_other, sibling, preferred_element_type=jnp.float32
    )
    branch_out = branch_out[:, :d_model]
    mixed = (residual + branch_out).astype(jnp.bfloat16)
    parts = jnp.stack(head_parts, 0)
    coeff_parts = jnp.einsum("tk,pkc->ptc", mixed, parts, preferred_element_type=jnp.float32).astype(
        jnp.bfloat16
    )
    order = me ^ jnp.arange(n_src, dtype=jnp.int32)
    coeffs = jnp.take(coeff_parts, order, axis=0).transpose(1, 0, 2).reshape(token_count, -1)
    tile_count = token_count // PATCH
    spec_rows = (
        coeffs.reshape(tile_count, GRID, GRID, 6, 2, SUB, SUB)
        .transpose(0, 1, 5, 3, 4, 2, 6)
        .reshape(tile_count, ORD, 12 * ORD)
    )
    return imaging(spec_rows, source_index, source_cutoff, source_weight)


def solution(mesh):
    return jax.shard_map(
        local,
        mesh=mesh,
        in_specs=(
            P(("tile", "src"), None),
            P(),
            P("tile", None),
            P("tile", None),
            P(None, "src"),
            P(),
            P(),
            P(),
        ),
        out_specs=P(("tile", "src"), None),
        check_vma=False,
    )
```

```python
import functools
import math

import jax
import jax.numpy as jnp
from jax import lax
from jax.experimental import pallas as pl
from jax.experimental.pallas import tpu as pltpu
from jax.sharding import PartitionSpec as P

GRID = 16
SUB = 8
W = 32
REG = 64
PIX = 64
SRC_DEV = 4
PATCH = 256
ORD = 128
f32 = jnp.float32
bf16 = jnp.bfloat16


def split_bf16(x):
    hi = lax.reduce_precision(x, exponent_bits=8, mantissa_bits=7)
    lo = x - hi
    return hi.astype(bf16), lo.astype(bf16)


def phase_tables():
    turn = 2.0 * math.pi / PIX
    v = jnp.arange(ORD, dtype=jnp.int32)
    y = jnp.arange(PIX, dtype=jnp.int32)
    ang = jnp.mod(v[:, None] * y[None, :], PIX).astype(f32) * turn
    cv, sv = jnp.cos(ang), jnp.sin(ang)
    t1 = jnp.concatenate([jnp.concatenate([cv, sv], 1), jnp.concatenate([-sv, cv], 1)], 0)
    i = jnp.arange(W, dtype=jnp.int32)
    x = jnp.arange(PIX, dtype=jnp.int32)
    ang2 = jnp.mod(x[:, None] * i[None, :], PIX).astype(f32) * turn
    t2 = jnp.concatenate([jnp.cos(ang2), jnp.sin(ang2)], 0)
    return t1, t2


def power_kernel(w_ref, *refs, sb):
    wm_refs, (t1_ref, t2_ref, out_ref, rcat) = refs[:6], refs[6:]
    step = pl.program_id(0)
    rcat[3 * W:, :] = jnp.zeros((W, sb * 6 * 2 * PIX), bf16)
    for k in range(6):
        x = wm_refs[k][...].reshape(sb * W, 2 * ORD)
        y = jnp.dot(x, t1_ref[...], preferred_element_type=f32)
        h = y[:, : 2 * PIX] + y[:, 2 * PIX:]
        hh = h.astype(bf16)
        hl = (h - hh.astype(f32)).astype(bf16)
        for j in range(sb):
            n = k * sb + j
            cols = slice(n * 2 * PIX, (n + 1) * 2 * PIX)
            rows = slice(j * W, (j + 1) * W)
            rcat[0:W, cols] = hh[rows, :]
            rcat[W:2 * W, cols] = hl[rows, :]
            rcat[2 * W:3 * W, cols] = hh[rows, :]
    q = jnp.dot(t2_ref[...], rcat[...], preferred_element_type=f32)
    acc = jnp.zeros((PIX, 2 * PIX), f32)
    for j in range(sb):
        part = jnp.zeros((PIX, 2 * PIX), f32)
        for k in range(6):
            n = k * sb + j
            blk = q[:, n * 2 * PIX:(n + 1) * 2 * PIX]
            rolled = pltpu.roll(blk, PIX, 1)
            er = blk[:PIX] - rolled[PIX:]
            ei = blk[PIX:] + rolled[:PIX]
            part = part + er * er + ei * ei
        acc = acc + w_ref[step * sb + j] * part

    @pl.when(step == 0)
    def _():
        out_ref[...] = jnp.zeros_like(out_ref)

    out_ref[...] += acc


def imaging(spec_rows, source_index, source_cutoff, source_weight, sb=8):
    T = spec_rows.shape[0]
    S = source_index.shape[0]
    x0 = jnp.clip(source_index[:, 0], 0, ORD - W)
    y0 = jnp.clip(source_index[:, 1], 0, ORD - W)
    rows = x0[:, None] + jnp.arange(W, dtype=jnp.int32)[None, :]
    pick = (rows[:, :, None] == jnp.arange(ORD, dtype=jnp.int32)[None, None, :]).astype(bf16)
    i = jnp.arange(W, dtype=jnp.int32)
    j = jnp.arange(12 * ORD, dtype=jnp.int32)[None, :] % ORD - y0[:, None]
    dist = (i[None, :, None] - W // 2) ** 2 + (j[:, None, :] - W // 2) ** 2
    keep = (dist <= (source_cutoff * source_cutoff)[:, None, None]) & (j[:, None, :] >= 0) & (j[:, None, :] < W)
    t1, t2 = phase_tables()
    t1h, t1l = split_bf16(t1)
    t1s = jnp.concatenate([t1h, t1l], 1)
    t2h, t2l = split_bf16(t2)
    t2c = jnp.concatenate([t2h, t2h, t2l, jnp.zeros((2 * PIX, W), bf16)], 1)
    blocks = [pl.BlockSpec((sb, W, 2 * ORD), functools.partial(lambda k, s: (s, 0, k), k)) for k in range(6)]
    call = pl.pallas_call(
        functools.partial(power_kernel, sb=sb),
        out_shape=jax.ShapeDtypeStruct((PIX, 2 * PIX), f32),
        grid=(S // sb,),
        in_specs=[pl.BlockSpec(memory_space=pltpu.SMEM)]
        + blocks
        + [
            pl.BlockSpec((2 * ORD, 4 * PIX), lambda s: (0, 0)),
            pl.BlockSpec((2 * PIX, 4 * W), lambda s: (0, 0)),
        ],
        out_specs=pl.BlockSpec((PIX, 2 * PIX), lambda s: (0, 0)),
        scratch_shapes=[pltpu.VMEM((4 * W, sb * 6 * 2 * PIX), bf16)],
        compiler_params=pltpu.CompilerParams(dimension_semantics=("arbitrary",)),
    )
    outs = []
    for t in range(T):
        strips = jnp.einsum("siu,un->sin", pick, spec_rows[t], preferred_element_type=f32)
        windows = jnp.where(keep, strips, 0.0).astype(bf16)
        outs.append(call(source_weight.astype(f32), *([windows] * 6), t1s, t2c)[:, :PIX])
    power = jnp.stack(outs, 0)
    return power.reshape(T, PIX * PIX) * (1.0 / (6.0 * W * W * S))


def local(
    tile_tokens,
    norm_gain,
    up_weight,
    down_weight,
    head_weight,
    source_index,
    source_cutoff,
    source_weight,
):
    token_count, d_model = tile_tokens.shape
    n_tile = lax.axis_size("tile")
    n_src = lax.axis_size("src")
    me = lax.axis_index("src")
    half = me % 2
    up_rows, ff = up_weight.shape
    down_rows = down_weight.shape[0]
    up_half, down_half = up_rows // 2, down_rows // 2
    depth = -(-(up_half + down_half) // 16) * 16
    width = max(ff, d_model)
    up_part = lax.dynamic_slice_in_dim(up_weight, half * up_half, up_half, 0)
    down_part = lax.dynamic_slice_in_dim(down_weight, half * down_half, down_half, 0)
    packed = jnp.concatenate(
        [
            jnp.pad(up_part, ((0, 0), (0, width - ff))),
            jnp.pad(down_part, ((0, depth - up_half - down_half), (0, width - d_model))),
        ],
        0,
    )
    gathered = lax.all_gather(packed, "tile", axis=0, tiled=True)
    sibling = lax.ppermute(gathered, "src", [(s, s ^ 1) for s in range(n_src)])
    head_parts = [head_weight] + [
        lax.ppermute(head_weight, "src", [(s, s ^ k) for s in range(n_src)]) for k in range(1, n_src)
    ]

    residual = tile_tokens.astype(jnp.float32)
    mean_square = jnp.mean(residual * residual, axis=1, keepdims=True)
    normed = (residual * lax.rsqrt(mean_square + 1e-05) * norm_gain).astype(jnp.bfloat16)

    def spread(x, rows, start):
        view = x.reshape(x.shape[0], n_tile, 2, rows // 2)
        pad = ((0, 0), (0, 0), (start, depth - start - rows // 2))
        mine = jnp.pad(lax.dynamic_index_in_dim(view, half, 2, keepdims=False), pad)
        other = jnp.pad(lax.dynamic_index_in_dim(view, 1 - half, 2, keepdims=False), pad)
        return mine.reshape(x.shape[0], -1), other.reshape(x.shape[0], -1)

    normed_mine, normed_other = spread(normed, up_rows, 0)
    pre_act = jnp.dot(normed_mine, gathered, preferred_element_type=jnp.float32) + jnp.dot(
        normed_other, sibling, preferred_element_type=jnp.float32
    )
    hidden = jax.nn.gelu(pre_act[:, :ff]).astype(jnp.bfloat16)
    hidden_mine, hidden_other = spread(hidden, down_rows, up_half)
    branch_out = jnp.dot(hidden_mine, gathered, preferred_element_type=jnp.float32) + jnp.dot(
        hidden_other, sibling, preferred_element_type=jnp.float32
    )
    branch_out = branch_out[:, :d_model]
    mixed = (residual + branch_out).astype(jnp.bfloat16)
    parts = jnp.stack(head_parts, 0)
    coeff_parts = jnp.einsum("tk,pkc->ptc", mixed, parts, preferred_element_type=jnp.float32).astype(
        jnp.bfloat16
    )
    order = me ^ jnp.arange(n_src, dtype=jnp.int32)
    coeffs = jnp.take(coeff_parts, order, axis=0).transpose(1, 0, 2).reshape(token_count, -1)
    tile_count = token_count // PATCH
    spec_rows = (
        coeffs.reshape(tile_count, GRID, GRID, 6, 2, SUB, SUB)
        .transpose(0, 1, 5, 3, 4, 2, 6)
        .reshape(tile_count, ORD, 12 * ORD)
    )
    return imaging(spec_rows, source_index, source_cutoff, source_weight)


def solution(mesh):
    return jax.shard_map(
        local,
        mesh=mesh,
        in_specs=(
            P(("tile", "src"), None),
            P(),
            P("tile", None),
            P("tile", None),
            P(None, "src"),
            P(),
            P(),
            P(),
        ),
        out_specs=P(("tile", "src"), None),
        check_vma=False,
    )
```

```python
import functools
import math

import jax
import jax.numpy as jnp
from jax import lax
from jax.experimental import pallas as pl
from jax.experimental.pallas import tpu as pltpu
from jax.sharding import PartitionSpec as P

GRID = 16
SUB = 8
W = 32
REG = 64
PIX = 64
SRC_DEV = 4
PATCH = 256
ORD = 128
f32 = jnp.float32
bf16 = jnp.bfloat16


def split_bf16(x):
    hi = lax.reduce_precision(x, exponent_bits=8, mantissa_bits=7)
    lo = x - hi
    return hi.astype(bf16), lo.astype(bf16)


def phase_tables():
    turn = 2.0 * math.pi / PIX
    v = jnp.arange(ORD, dtype=jnp.int32)
    y = jnp.arange(PIX, dtype=jnp.int32)
    ang = jnp.mod(v[:, None] * y[None, :], PIX).astype(f32) * turn
    cv, sv = jnp.cos(ang), jnp.sin(ang)
    t1 = jnp.concatenate([jnp.concatenate([cv, sv], 1), jnp.concatenate([-sv, cv], 1)], 0)
    i = jnp.arange(W, dtype=jnp.int32)
    x = jnp.arange(PIX, dtype=jnp.int32)
    ang2 = jnp.mod(x[:, None] * i[None, :], PIX).astype(f32) * turn
    t2 = jnp.concatenate([jnp.cos(ang2), jnp.sin(ang2)], 0)
    return t1, t2


def power_kernel(w_ref, *refs, sb):
    wm_refs, (t1_ref, t2_ref, out_ref, rcat) = refs[:6], refs[6:]
    step = pl.program_id(0)
    rcat[3 * W:, :] = jnp.zeros((W, sb * 6 * 2 * PIX), bf16)
    for k in range(6):
        x = wm_refs[k][...].reshape(sb * W, 2 * ORD)
        y = jnp.dot(x, t1_ref[...], preferred_element_type=f32)
        h = y[:, : 2 * PIX] + y[:, 2 * PIX:]
        hh = h.astype(bf16)
        hl = (h - hh.astype(f32)).astype(bf16)
        for j in range(sb):
            n = k * sb + j
            cols = slice(n * 2 * PIX, (n + 1) * 2 * PIX)
            rows = slice(j * W, (j + 1) * W)
            rcat[0:W, cols] = hh[rows, :]
            rcat[W:2 * W, cols] = hl[rows, :]
            rcat[2 * W:3 * W, cols] = hh[rows, :]
    q = jnp.dot(t2_ref[...], rcat[...], preferred_element_type=f32)
    acc = jnp.zeros((PIX, 2 * PIX), f32)
    for j in range(sb):
        part = jnp.zeros((PIX, 2 * PIX), f32)
        for k in range(6):
            n = k * sb + j
            blk = q[:, n * 2 * PIX:(n + 1) * 2 * PIX]
            rolled = pltpu.roll(blk, PIX, 1)
            er = blk[:PIX] - rolled[PIX:]
            ei = blk[PIX:] + rolled[:PIX]
            part = part + er * er + ei * ei
        acc = acc + w_ref[step * sb + j] * part

    @pl.when(step == 0)
    def _():
        out_ref[...] = jnp.zeros_like(out_ref)

    out_ref[...] += acc


def imaging(spec_rows, source_index, source_cutoff, source_weight, sb=8):
    T = spec_rows.shape[0]
    S = source_index.shape[0]
    x0 = jnp.clip(source_index[:, 0], 0, ORD - W)
    y0 = jnp.clip(source_index[:, 1], 0, ORD - W)
    rows = x0[:, None] + jnp.arange(W, dtype=jnp.int32)[None, :]
    pick = (rows[:, :, None] == jnp.arange(ORD, dtype=jnp.int32)[None, None, :]).astype(bf16)
    i = jnp.arange(W, dtype=jnp.int32)
    n = jnp.arange(12 * ORD, dtype=jnp.int32)
    j = ((n % GRID) * SUB + (n % ORD) // GRID)[None, :] - y0[:, None]
    dist = (i[None, :, None] - W // 2) ** 2 + (j[:, None, :] - W // 2) ** 2
    keep = (dist <= (source_cutoff * source_cutoff)[:, None, None]) & (j[:, None, :] >= 0) & (j[:, None, :] < W)
    t1, t2 = phase_tables()
    t1 = t1.reshape(2, GRID, SUB, 2 * PIX).transpose(0, 2, 1, 3).reshape(2 * ORD, 2 * PIX)
    t1h, t1l = split_bf16(t1)
    t1s = jnp.concatenate([t1h, t1l], 1)
    t2h, t2l = split_bf16(t2)
    t2c = jnp.concatenate([t2h, t2h, t2l, jnp.zeros((2 * PIX, W), bf16)], 1)
    blocks = [pl.BlockSpec((sb, W, 2 * ORD), functools.partial(lambda k, s: (s, 0, k), k)) for k in range(6)]
    call = pl.pallas_call(
        functools.partial(power_kernel, sb=sb),
        out_shape=jax.ShapeDtypeStruct((PIX, 2 * PIX), f32),
        grid=(S // sb,),
        in_specs=[pl.BlockSpec(memory_space=pltpu.SMEM)]
        + blocks
        + [
            pl.BlockSpec((2 * ORD, 4 * PIX), lambda s: (0, 0)),
            pl.BlockSpec((2 * PIX, 4 * W), lambda s: (0, 0)),
        ],
        out_specs=pl.BlockSpec((PIX, 2 * PIX), lambda s: (0, 0)),
        scratch_shapes=[pltpu.VMEM((4 * W, sb * 6 * 2 * PIX), bf16)],
        compiler_params=pltpu.CompilerParams(dimension_semantics=("arbitrary",)),
    )
    outs = []
    for t in range(T):
        strips = jnp.einsum("siu,un->sin", pick, spec_rows[t], preferred_element_type=f32)
        windows = jnp.where(keep, strips, 0.0).astype(bf16)
        outs.append(call(source_weight.astype(f32), *([windows] * 6), t1s, t2c)[:, :PIX])
    power = jnp.stack(outs, 0)
    return power.reshape(T, PIX * PIX) * (1.0 / (6.0 * W * W * S))


def local(
    tile_tokens,
    norm_gain,
    up_weight,
    down_weight,
    head_weight,
    source_index,
    source_cutoff,
    source_weight,
):
    token_count, d_model = tile_tokens.shape
    n_tile = lax.axis_size("tile")
    n_src = lax.axis_size("src")
    me = lax.axis_index("src")
    half = me % 2
    up_rows, ff = up_weight.shape
    down_rows = down_weight.shape[0]
    up_half, down_half = up_rows // 2, down_rows // 2
    depth = -(-(up_half + down_half) // 16) * 16
    width = max(ff, d_model)
    up_part = lax.dynamic_slice_in_dim(up_weight, half * up_half, up_half, 0)
    down_part = lax.dynamic_slice_in_dim(down_weight, half * down_half, down_half, 0)
    packed = jnp.concatenate(
        [
            jnp.pad(up_part, ((0, 0), (0, width - ff))),
            jnp.pad(down_part, ((0, depth - up_half - down_half), (0, width - d_model))),
        ],
        0,
    )
    gathered = lax.all_gather(packed, "tile", axis=0, tiled=True)
    sibling = lax.ppermute(gathered, "src", [(s, s ^ 1) for s in range(n_src)])
    head_parts = [head_weight] + [
        lax.ppermute(head_weight, "src", [(s, s ^ k) for s in range(n_src)]) for k in range(1, n_src)
    ]

    residual = tile_tokens.astype(jnp.float32)
    mean_square = jnp.mean(residual * residual, axis=1, keepdims=True)
    normed = (residual * lax.rsqrt(mean_square + 1e-05) * norm_gain).astype(jnp.bfloat16)

    def spread(x, rows, start):
        view = x.reshape(x.shape[0], n_tile, 2, rows // 2)
        pad = ((0, 0), (0, 0), (start, depth - start - rows // 2))
        mine = jnp.pad(lax.dynamic_index_in_dim(view, half, 2, keepdims=False), pad)
        other = jnp.pad(lax.dynamic_index_in_dim(view, 1 - half, 2, keepdims=False), pad)
        return mine.reshape(x.shape[0], -1), other.reshape(x.shape[0], -1)

    normed_mine, normed_other = spread(normed, up_rows, 0)
    pre_act = jnp.dot(normed_mine, gathered, preferred_element_type=jnp.float32) + jnp.dot(
        normed_other, sibling, preferred_element_type=jnp.float32
    )
    hidden = jax.nn.gelu(pre_act[:, :ff]).astype(jnp.bfloat16)
    hidden_mine, hidden_other = spread(hidden, down_rows, up_half)
    branch_out = jnp.dot(hidden_mine, gathered, preferred_element_type=jnp.float32) + jnp.dot(
        hidden_other, sibling, preferred_element_type=jnp.float32
    )
    branch_out = branch_out[:, :d_model]
    mixed = (residual + branch_out).astype(jnp.bfloat16)
    parts = jnp.stack(head_parts, 0)
    coeff_parts = jnp.einsum("tk,pkc->ptc", mixed, parts, preferred_element_type=jnp.float32).astype(
        jnp.bfloat16
    )
    order = me ^ jnp.arange(n_src, dtype=jnp.int32)
    coeffs = jnp.take(coeff_parts, order, axis=0).transpose(1, 0, 2).reshape(token_count, -1)
    tile_count = token_count // PATCH
    spec_rows = (
        coeffs.reshape(tile_count, GRID, GRID, 6, 2, SUB, SUB)
        .transpose(0, 1, 5, 3, 4, 6, 2)
        .reshape(tile_count, ORD, 12 * ORD)
    )
    return imaging(spec_rows, source_index, source_cutoff, source_weight)


def solution(mesh):
    return jax.shard_map(
        local,
        mesh=mesh,
        in_specs=(
            P(("tile", "src"), None),
            P(),
            P("tile", None),
            P("tile", None),
            P(None, "src"),
            P(),
            P(),
            P(),
        ),
        out_specs=P(("tile", "src"), None),
        check_vma=False,
    )
```

```python
import functools
import math

import jax
import jax.numpy as jnp
from jax import lax
from jax.experimental import pallas as pl
from jax.experimental.pallas import tpu as pltpu
from jax.sharding import PartitionSpec as P

GRID = 16
SUB = 8
W = 32
REG = 64
PIX = 64
SRC_DEV = 4
PATCH = 256
ORD = 128
f32 = jnp.float32
bf16 = jnp.bfloat16


def split_bf16(x):
    hi = lax.reduce_precision(x, exponent_bits=8, mantissa_bits=7)
    lo = x - hi
    return hi.astype(bf16), lo.astype(bf16)


def phase_tables():
    turn = 2.0 * math.pi / PIX
    v = jnp.arange(ORD, dtype=jnp.int32)
    y = jnp.arange(PIX, dtype=jnp.int32)
    ang = jnp.mod(v[:, None] * y[None, :], PIX).astype(f32) * turn
    cv, sv = jnp.cos(ang), jnp.sin(ang)
    t1 = jnp.concatenate([jnp.concatenate([cv, sv], 1), jnp.concatenate([-sv, cv], 1)], 0)
    i = jnp.arange(W, dtype=jnp.int32)
    x = jnp.arange(PIX, dtype=jnp.int32)
    ang2 = jnp.mod(x[:, None] * i[None, :], PIX).astype(f32) * turn
    t2 = jnp.concatenate([jnp.cos(ang2), jnp.sin(ang2)], 0)
    return t1, t2


def power_kernel(w_ref, *refs, sb):
    wm_refs, (t1_ref, t2_ref, out_ref, rcat) = refs[:6], refs[6:]
    step = pl.program_id(0)
    rcat[3 * W:, :] = jnp.zeros((W, sb * 6 * 2 * PIX), bf16)
    for k in range(6):
        x = wm_refs[k][...].reshape(sb * W, 2 * ORD)
        y = jnp.dot(x, t1_ref[...], preferred_element_type=f32)
        h = y[:, : 2 * PIX] + y[:, 2 * PIX:]
        hh = h.astype(bf16)
        hl = (h - hh.astype(f32)).astype(bf16)
        for j in range(sb):
            n = k * sb + j
            cols = slice(n * 2 * PIX, (n + 1) * 2 * PIX)
            rows = slice(j * W, (j + 1) * W)
            rcat[0:W, cols] = hh[rows, :]
            rcat[W:2 * W, cols] = hl[rows, :]
            rcat[2 * W:3 * W, cols] = hh[rows, :]
    q = jnp.dot(t2_ref[...], rcat[...], preferred_element_type=f32)
    acc = jnp.zeros((PIX, 2 * PIX), f32)
    for j in range(sb):
        part = jnp.zeros((PIX, 2 * PIX), f32)
        for k in range(6):
            n = k * sb + j
            blk = q[:, n * 2 * PIX:(n + 1) * 2 * PIX]
            rolled = pltpu.roll(blk, PIX, 1)
            er = blk[:PIX] - rolled[PIX:]
            ei = blk[PIX:] + rolled[:PIX]
            part = part + er * er + ei * ei
        acc = acc + w_ref[step * sb + j] * part

    @pl.when(step == 0)
    def _():
        out_ref[...] = jnp.zeros_like(out_ref)

    out_ref[...] += acc


def imaging(spec_rows, source_index, source_cutoff, source_weight, sb=16):
    T = spec_rows.shape[0]
    S = source_index.shape[0]
    x0 = jnp.clip(source_index[:, 0], 0, ORD - W)
    y0 = jnp.clip(source_index[:, 1], 0, ORD - W)
    rows = x0[:, None] + jnp.arange(W, dtype=jnp.int32)[None, :]
    pick = (rows[:, :, None] == jnp.arange(ORD, dtype=jnp.int32)[None, None, :]).astype(bf16)
    i = jnp.arange(W, dtype=jnp.int32)
    n = jnp.arange(12 * ORD, dtype=jnp.int32)
    j = ((n % GRID) * SUB + (n % ORD) // GRID)[None, :] - y0[:, None]
    dist = (i[None, :, None] - W // 2) ** 2 + (j[:, None, :] - W // 2) ** 2
    keep = (dist <= (source_cutoff * source_cutoff)[:, None, None]) & (j[:, None, :] >= 0) & (j[:, None, :] < W)
    t1, t2 = phase_tables()
    t1 = t1.reshape(2, GRID, SUB, 2 * PIX).transpose(0, 2, 1, 3).reshape(2 * ORD, 2 * PIX)
    t1h, t1l = split_bf16(t1)
    t1s = jnp.concatenate([t1h, t1l], 1)
    t2h, t2l = split_bf16(t2)
    t2c = jnp.concatenate([t2h, t2h, t2l, jnp.zeros((2 * PIX, W), bf16)], 1)
    blocks = [pl.BlockSpec((sb, W, 2 * ORD), functools.partial(lambda k, s: (s, 0, k), k)) for k in range(6)]
    call = pl.pallas_call(
        functools.partial(power_kernel, sb=sb),
        out_shape=jax.ShapeDtypeStruct((PIX, 2 * PIX), f32),
        grid=(S // sb,),
        in_specs=[pl.BlockSpec(memory_space=pltpu.SMEM)]
        + blocks
        + [
            pl.BlockSpec((2 * ORD, 4 * PIX), lambda s: (0, 0)),
            pl.BlockSpec((2 * PIX, 4 * W), lambda s: (0, 0)),
        ],
        out_specs=pl.BlockSpec((PIX, 2 * PIX), lambda s: (0, 0)),
        scratch_shapes=[pltpu.VMEM((4 * W, sb * 6 * 2 * PIX), bf16)],
        compiler_params=pltpu.CompilerParams(dimension_semantics=("arbitrary",)),
    )
    outs = []
    for t in range(T):
        strips = jnp.einsum("siu,un->sin", pick, spec_rows[t], preferred_element_type=f32)
        windows = jnp.where(keep, strips, 0.0).astype(bf16)
        outs.append(call(source_weight.astype(f32), *([windows] * 6), t1s, t2c)[:, :PIX])
    power = jnp.stack(outs, 0)
    return power.reshape(T, PIX * PIX) * (1.0 / (6.0 * W * W * S))


def local(
    tile_tokens,
    norm_gain,
    up_weight,
    down_weight,
    head_weight,
    source_index,
    source_cutoff,
    source_weight,
):
    token_count, d_model = tile_tokens.shape
    n_tile = lax.axis_size("tile")
    n_src = lax.axis_size("src")
    me = lax.axis_index("src")
    half = me % 2
    up_rows, ff = up_weight.shape
    down_rows = down_weight.shape[0]
    up_half, down_half = up_rows // 2, down_rows // 2
    depth = -(-(up_half + down_half) // 16) * 16
    width = max(ff, d_model)
    up_part = lax.dynamic_slice_in_dim(up_weight, half * up_half, up_half, 0)
    down_part = lax.dynamic_slice_in_dim(down_weight, half * down_half, down_half, 0)
    packed = jnp.concatenate(
        [
            jnp.pad(up_part, ((0, 0), (0, width - ff))),
            jnp.pad(down_part, ((0, depth - up_half - down_half), (0, width - d_model))),
        ],
        0,
    )
    gathered = lax.all_gather(packed, "tile", axis=0, tiled=True)
    sibling = lax.ppermute(gathered, "src", [(s, s ^ 1) for s in range(n_src)])
    head_parts = [head_weight] + [
        lax.ppermute(head_weight, "src", [(s, s ^ k) for s in range(n_src)]) for k in range(1, n_src)
    ]

    residual = tile_tokens.astype(jnp.float32)
    mean_square = jnp.mean(residual * residual, axis=1, keepdims=True)
    normed = (residual * lax.rsqrt(mean_square + 1e-05) * norm_gain).astype(jnp.bfloat16)

    def spread(x, rows, start):
        view = x.reshape(x.shape[0], n_tile, 2, rows // 2)
        pad = ((0, 0), (0, 0), (start, depth - start - rows // 2))
        mine = jnp.pad(lax.dynamic_index_in_dim(view, half, 2, keepdims=False), pad)
        other = jnp.pad(lax.dynamic_index_in_dim(view, 1 - half, 2, keepdims=False), pad)
        return mine.reshape(x.shape[0], -1), other.reshape(x.shape[0], -1)

    normed_mine, normed_other = spread(normed, up_rows, 0)
    pre_act = jnp.dot(normed_mine, gathered, preferred_element_type=jnp.float32) + jnp.dot(
        normed_other, sibling, preferred_element_type=jnp.float32
    )
    hidden = jax.nn.gelu(pre_act[:, :ff]).astype(jnp.bfloat16)
    hidden_mine, hidden_other = spread(hidden, down_rows, up_half)
    branch_out = jnp.dot(hidden_mine, gathered, preferred_element_type=jnp.float32) + jnp.dot(
        hidden_other, sibling, preferred_element_type=jnp.float32
    )
    branch_out = branch_out[:, :d_model]
    mixed = (residual + branch_out).astype(jnp.bfloat16)
    parts = jnp.stack(head_parts, 0)
    coeff_parts = jnp.einsum("tk,pkc->ptc", mixed, parts, preferred_element_type=jnp.float32).astype(
        jnp.bfloat16
    )
    order = me ^ jnp.arange(n_src, dtype=jnp.int32)
    coeffs = jnp.take(coeff_parts, order, axis=0).transpose(1, 0, 2).reshape(token_count, -1)
    tile_count = token_count // PATCH
    spec_rows = (
        coeffs.reshape(tile_count, GRID, GRID, 6, 2, SUB, SUB)
        .transpose(0, 1, 5, 3, 4, 6, 2)
        .reshape(tile_count, ORD, 12 * ORD)
    )
    return imaging(spec_rows, source_index, source_cutoff, source_weight)


def solution(mesh):
    return jax.shard_map(
        local,
        mesh=mesh,
        in_specs=(
            P(("tile", "src"), None),
            P(),
            P("tile", None),
            P("tile", None),
            P(None, "src"),
            P(),
            P(),
            P(),
        ),
        out_specs=P(("tile", "src"), None),
        check_vma=False,
    )
```

```python
import functools
import math

import jax
import jax.numpy as jnp
from jax import lax
from jax.experimental import pallas as pl
from jax.experimental.pallas import tpu as pltpu
from jax.sharding import PartitionSpec as P

GRID = 16
SUB = 8
W = 32
REG = 64
PIX = 64
SRC_DEV = 4
PATCH = 256
ORD = 128
f32 = jnp.float32
bf16 = jnp.bfloat16


def split_bf16(x):
    hi = lax.reduce_precision(x, exponent_bits=8, mantissa_bits=7)
    lo = x - hi
    return hi.astype(bf16), lo.astype(bf16)


def phase_tables():
    turn = 2.0 * math.pi / PIX
    v = jnp.arange(ORD, dtype=jnp.int32)
    y = jnp.arange(PIX, dtype=jnp.int32)
    ang = jnp.mod(v[:, None] * y[None, :], PIX).astype(f32) * turn
    cv, sv = jnp.cos(ang), jnp.sin(ang)
    t1 = jnp.concatenate([jnp.concatenate([cv, sv], 1), jnp.concatenate([-sv, cv], 1)], 0)
    i = jnp.arange(W, dtype=jnp.int32)
    x = jnp.arange(PIX, dtype=jnp.int32)
    ang2 = jnp.mod(x[:, None] * i[None, :], PIX).astype(f32) * turn
    t2 = jnp.concatenate([jnp.cos(ang2), jnp.sin(ang2)], 0)
    return t1, t2


def power_kernel(w_ref, x0_ref, y0_ref, r_ref, spec_ref, t1_ref, t2_ref, out_ref, xs, rcat, *, sb):
    step = pl.program_id(0)
    rcat[3 * W:, :] = jnp.zeros((W, sb * 6 * 2 * PIX), bf16)
    n = lax.broadcasted_iota(jnp.int32, (W, 2 * ORD), 1)
    col = (n % GRID) * SUB + (n % ORD) // GRID
    row = lax.broadcasted_iota(jnp.int32, (W, 2 * ORD), 0)
    keeps = []
    for j in range(sb):
        s = step * sb + j
        jj = col - y0_ref[s]
        radius = r_ref[s]
        keep = ((row - W // 2) ** 2 + (jj - W // 2) ** 2 <= radius * radius) & (jj >= 0) & (jj < W)
        keeps.append(keep)
    for k in range(6):
        for j in range(sb):
            s = step * sb + j
            start = x0_ref[s]
            base = pl.multiple_of((start // 8) * 8, 8)
            wide = spec_ref[pl.ds(base, W + 8), pl.ds(k * 2 * ORD, 2 * ORD)]
            rows = pltpu.roll(wide, (W + 8 - (start - base)) % (W + 8), 0)[:W]
            xs[j * W:(j + 1) * W, :] = jnp.where(keeps[j], rows, 0.0).astype(bf16)
        y = jnp.dot(xs[...], t1_ref[...], preferred_element_type=f32)
        h = y[:, : 2 * PIX] + y[:, 2 * PIX:]
        hh = h.astype(bf16)
        hl = (h - hh.astype(f32)).astype(bf16)
        for j in range(sb):
            m = k * sb + j
            cols = slice(m * 2 * PIX, (m + 1) * 2 * PIX)
            rows_ = slice(j * W, (j + 1) * W)
            rcat[0:W, cols] = hh[rows_, :]
            rcat[W:2 * W, cols] = hl[rows_, :]
            rcat[2 * W:3 * W, cols] = hh[rows_, :]
    q = jnp.dot(t2_ref[...], rcat[...], preferred_element_type=f32)
    acc = jnp.zeros((PIX, 2 * PIX), f32)
    for j in range(sb):
        part = jnp.zeros((PIX, 2 * PIX), f32)
        for k in range(6):
            m = k * sb + j
            blk = q[:, m * 2 * PIX:(m + 1) * 2 * PIX]
            rolled = pltpu.roll(blk, PIX, 1)
            er = blk[:PIX] - rolled[PIX:]
            ei = blk[PIX:] + rolled[:PIX]
            part = part + er * er + ei * ei
        acc = acc + w_ref[step * sb + j] * part

    @pl.when(step == 0)
    def _():
        out_ref[...] = jnp.zeros_like(out_ref)

    out_ref[...] += acc


def imaging(spec_rows, source_index, source_cutoff, source_weight, sb=16):
    T = spec_rows.shape[0]
    S = source_index.shape[0]
    x0 = jnp.clip(source_index[:, 0], 0, ORD - W)
    y0 = jnp.clip(source_index[:, 1], 0, ORD - W)
    t1, t2 = phase_tables()
    t1 = t1.reshape(2, GRID, SUB, 2 * PIX).transpose(0, 2, 1, 3).reshape(2 * ORD, 2 * PIX)
    t1h, t1l = split_bf16(t1)
    t1s = jnp.concatenate([t1h, t1l], 1)
    t2h, t2l = split_bf16(t2)
    t2c = jnp.concatenate([t2h, t2h, t2l, jnp.zeros((2 * PIX, W), bf16)], 1)
    smem = pl.BlockSpec(memory_space=pltpu.SMEM)
    call = pl.pallas_call(
        functools.partial(power_kernel, sb=sb),
        out_shape=jax.ShapeDtypeStruct((PIX, 2 * PIX), f32),
        grid=(S // sb,),
        in_specs=[smem] * 4
        + [
            pl.BlockSpec((ORD + 8, 12 * ORD), lambda s: (0, 0)),
            pl.BlockSpec((2 * ORD, 4 * PIX), lambda s: (0, 0)),
            pl.BlockSpec((2 * PIX, 4 * W), lambda s: (0, 0)),
        ],
        out_specs=pl.BlockSpec((PIX, 2 * PIX), lambda s: (0, 0)),
        scratch_shapes=[pltpu.VMEM((sb * W, 2 * ORD), bf16), pltpu.VMEM((4 * W, sb * 6 * 2 * PIX), bf16)],
        compiler_params=pltpu.CompilerParams(dimension_semantics=("arbitrary",)),
    )
    outs = []
    for t in range(T):
        outs.append(
            call(
                source_weight.astype(f32), x0, y0, source_cutoff, jnp.pad(spec_rows[t].astype(f32), ((0, 8), (0, 0))), t1s, t2c
            )[:, :PIX]
        )
    power = jnp.stack(outs, 0)
    return power.reshape(T, PIX * PIX) * (1.0 / (6.0 * W * W * S))


def local(
    tile_tokens,
    norm_gain,
    up_weight,
    down_weight,
    head_weight,
    source_index,
    source_cutoff,
    source_weight,
):
    token_count, d_model = tile_tokens.shape
    n_tile = lax.axis_size("tile")
    n_src = lax.axis_size("src")
    me = lax.axis_index("src")
    half = me % 2
    up_rows, ff = up_weight.shape
    down_rows = down_weight.shape[0]
    up_half, down_half = up_rows // 2, down_rows // 2
    depth = -(-(up_half + down_half) // 16) * 16
    width = max(ff, d_model)
    up_part = lax.dynamic_slice_in_dim(up_weight, half * up_half, up_half, 0)
    down_part = lax.dynamic_slice_in_dim(down_weight, half * down_half, down_half, 0)
    packed = jnp.concatenate(
        [
            jnp.pad(up_part, ((0, 0), (0, width - ff))),
            jnp.pad(down_part, ((0, depth - up_half - down_half), (0, width - d_model))),
        ],
        0,
    )
    gathered = lax.all_gather(packed, "tile", axis=0, tiled=True)
    sibling = lax.ppermute(gathered, "src", [(s, s ^ 1) for s in range(n_src)])
    head_parts = [head_weight] + [
        lax.ppermute(head_weight, "src", [(s, s ^ k) for s in range(n_src)]) for k in range(1, n_src)
    ]

    residual = tile_tokens.astype(jnp.float32)
    mean_square = jnp.mean(residual * residual, axis=1, keepdims=True)
    normed = (residual * lax.rsqrt(mean_square + 1e-05) * norm_gain).astype(jnp.bfloat16)

    def spread(x, rows, start):
        view = x.reshape(x.shape[0], n_tile, 2, rows // 2)
        pad = ((0, 0), (0, 0), (start, depth - start - rows // 2))
        mine = jnp.pad(lax.dynamic_index_in_dim(view, half, 2, keepdims=False), pad)
        other = jnp.pad(lax.dynamic_index_in_dim(view, 1 - half, 2, keepdims=False), pad)
        return mine.reshape(x.shape[0], -1), other.reshape(x.shape[0], -1)

    normed_mine, normed_other = spread(normed, up_rows, 0)
    pre_act = jnp.dot(normed_mine, gathered, preferred_element_type=jnp.float32) + jnp.dot(
        normed_other, sibling, preferred_element_type=jnp.float32
    )
    hidden = jax.nn.gelu(pre_act[:, :ff]).astype(jnp.bfloat16)
    hidden_mine, hidden_other = spread(hidden, down_rows, up_half)
    branch_out = jnp.dot(hidden_mine, gathered, preferred_element_type=jnp.float32) + jnp.dot(
        hidden_other, sibling, preferred_element_type=jnp.float32
    )
    branch_out = branch_out[:, :d_model]
    mixed = (residual + branch_out).astype(jnp.bfloat16)
    parts = jnp.stack(head_parts, 0)
    coeff_parts = jnp.einsum("tk,pkc->ptc", mixed, parts, preferred_element_type=jnp.float32).astype(
        jnp.bfloat16
    )
    order = me ^ jnp.arange(n_src, dtype=jnp.int32)
    coeffs = jnp.take(coeff_parts, order, axis=0).transpose(1, 0, 2).reshape(token_count, -1)
    tile_count = token_count // PATCH
    spec_rows = (
        coeffs.reshape(tile_count, GRID, GRID, 6, 2, SUB, SUB)
        .transpose(0, 1, 5, 3, 4, 6, 2)
        .reshape(tile_count, ORD, 12 * ORD)
    )
    return imaging(spec_rows, source_index, source_cutoff, source_weight)


def solution(mesh):
    return jax.shard_map(
        local,
        mesh=mesh,
        in_specs=(
            P(("tile", "src"), None),
            P(),
            P("tile", None),
            P("tile", None),
            P(None, "src"),
            P(),
            P(),
            P(),
        ),
        out_specs=P(("tile", "src"), None),
        check_vma=False,
    )
```

```python
import functools
import math

import jax
import jax.numpy as jnp
from jax import lax
from jax.experimental import pallas as pl
from jax.experimental.pallas import tpu as pltpu
from jax.sharding import PartitionSpec as P

GRID = 16
SUB = 8
W = 32
REG = 64
PIX = 64
SRC_DEV = 4
PATCH = 256
ORD = 128
f32 = jnp.float32
bf16 = jnp.bfloat16


def split_bf16(x):
    hi = lax.reduce_precision(x, exponent_bits=8, mantissa_bits=7)
    lo = x - hi
    return hi.astype(bf16), lo.astype(bf16)


def phase_tables():
    turn = 2.0 * math.pi / PIX
    v = jnp.arange(ORD, dtype=jnp.int32)
    y = jnp.arange(PIX, dtype=jnp.int32)
    ang = jnp.mod(v[:, None] * y[None, :], PIX).astype(f32) * turn
    cv, sv = jnp.cos(ang), jnp.sin(ang)
    t1 = jnp.concatenate([jnp.concatenate([cv, sv], 1), jnp.concatenate([-sv, cv], 1)], 0)
    i = jnp.arange(W, dtype=jnp.int32)
    x = jnp.arange(PIX, dtype=jnp.int32)
    ang2 = jnp.mod(x[:, None] * i[None, :], PIX).astype(f32) * turn
    t2 = jnp.concatenate([jnp.cos(ang2), jnp.sin(ang2)], 0)
    return t1, t2


def power_kernel(w_ref, x0_ref, y0_ref, r_ref, spec_ref, t1_ref, t2_ref, out_ref, xs, rcat, *, sb):
    step = pl.program_id(0)
    rcat[3 * W:, :] = jnp.zeros((W, sb * 6 * 2 * PIX), bf16)
    n = lax.broadcasted_iota(jnp.int32, (W, 2 * ORD), 1)
    col = (n % GRID) * SUB + (n % ORD) // GRID
    row = lax.broadcasted_iota(jnp.int32, (W, 2 * ORD), 0)
    keeps = []
    for j in range(sb):
        s = step * sb + j
        jj = col - y0_ref[s]
        radius = r_ref[s]
        keep = ((row - W // 2) ** 2 + (jj - W // 2) ** 2 <= radius * radius) & (jj >= 0) & (jj < W)
        keeps.append(keep)
    for k in range(6):
        for j in range(sb):
            s = step * sb + j
            start = x0_ref[s]
            base = pl.multiple_of((start // 16) * 16, 16)
            wide = spec_ref[pl.ds(base, W + 16), pl.ds(k * 2 * ORD, 2 * ORD)].astype(f32)
            rows = pltpu.roll(wide, (W + 16 - (start - base)) % (W + 16), 0)[:W]
            xs[j * W:(j + 1) * W, :] = jnp.where(keeps[j], rows, 0.0).astype(bf16)
        y = jnp.dot(xs[...], t1_ref[...], preferred_element_type=f32)
        h = y[:, : 2 * PIX] + y[:, 2 * PIX:]
        hh = h.astype(bf16)
        hl = (h - hh.astype(f32)).astype(bf16)
        for j in range(sb):
            m = k * sb + j
            cols = slice(m * 2 * PIX, (m + 1) * 2 * PIX)
            rows_ = slice(j * W, (j + 1) * W)
            rcat[0:W, cols] = hh[rows_, :]
            rcat[W:2 * W, cols] = hl[rows_, :]
            rcat[2 * W:3 * W, cols] = hh[rows_, :]
    q = jnp.dot(t2_ref[...], rcat[...], preferred_element_type=f32)
    acc = jnp.zeros((PIX, 2 * PIX), f32)
    for j in range(sb):
        part = jnp.zeros((PIX, 2 * PIX), f32)
        for k in range(6):
            m = k * sb + j
            blk = q[:, m * 2 * PIX:(m + 1) * 2 * PIX]
            rolled = pltpu.roll(blk, PIX, 1)
            er = blk[:PIX] - rolled[PIX:]
            ei = blk[PIX:] + rolled[:PIX]
            part = part + er * er + ei * ei
        acc = acc + w_ref[step * sb + j] * part

    @pl.when(step == 0)
    def _():
        out_ref[...] = jnp.zeros_like(out_ref)

    out_ref[...] += acc


def imaging(spec_rows, source_index, source_cutoff, source_weight, sb=16):
    T = spec_rows.shape[0]
    S = source_index.shape[0]
    x0 = jnp.clip(source_index[:, 0], 0, ORD - W)
    y0 = jnp.clip(source_index[:, 1], 0, ORD - W)
    t1, t2 = phase_tables()
    t1 = t1.reshape(2, GRID, SUB, 2 * PIX).transpose(0, 2, 1, 3).reshape(2 * ORD, 2 * PIX)
    t1h, t1l = split_bf16(t1)
    t1s = jnp.concatenate([t1h, t1l], 1)
    t2h, t2l = split_bf16(t2)
    t2c = jnp.concatenate([t2h, t2h, t2l, jnp.zeros((2 * PIX, W), bf16)], 1)
    smem = pl.BlockSpec(memory_space=pltpu.SMEM)
    call = pl.pallas_call(
        functools.partial(power_kernel, sb=sb),
        out_shape=jax.ShapeDtypeStruct((PIX, 2 * PIX), f32),
        grid=(S // sb,),
        in_specs=[smem] * 4
        + [
            pl.BlockSpec((ORD + 16, 12 * ORD), lambda s: (0, 0)),
            pl.BlockSpec((2 * ORD, 4 * PIX), lambda s: (0, 0)),
            pl.BlockSpec((2 * PIX, 4 * W), lambda s: (0, 0)),
        ],
        out_specs=pl.BlockSpec((PIX, 2 * PIX), lambda s: (0, 0)),
        scratch_shapes=[pltpu.VMEM((sb * W, 2 * ORD), bf16), pltpu.VMEM((4 * W, sb * 6 * 2 * PIX), bf16)],
        compiler_params=pltpu.CompilerParams(dimension_semantics=("arbitrary",)),
    )
    outs = []
    for t in range(T):
        outs.append(
            call(
                source_weight.astype(f32), x0, y0, source_cutoff, jnp.pad(spec_rows[t], ((0, 16), (0, 0))), t1s, t2c
            )[:, :PIX]
        )
    power = jnp.stack(outs, 0)
    return power.reshape(T, PIX * PIX) * (1.0 / (6.0 * W * W * S))


def local(
    tile_tokens,
    norm_gain,
    up_weight,
    down_weight,
    head_weight,
    source_index,
    source_cutoff,
    source_weight,
):
    token_count, d_model = tile_tokens.shape
    n_tile = lax.axis_size("tile")
    n_src = lax.axis_size("src")
    me = lax.axis_index("src")
    half = me % 2
    up_rows, ff = up_weight.shape
    down_rows = down_weight.shape[0]
    up_half, down_half = up_rows // 2, down_rows // 2
    depth = -(-(up_half + down_half) // 16) * 16
    width = max(ff, d_model)
    up_part = lax.dynamic_slice_in_dim(up_weight, half * up_half, up_half, 0)
    down_part = lax.dynamic_slice_in_dim(down_weight, half * down_half, down_half, 0)
    packed = jnp.concatenate(
        [
            jnp.pad(up_part, ((0, 0), (0, width - ff))),
            jnp.pad(down_part, ((0, depth - up_half - down_half), (0, width - d_model))),
        ],
        0,
    )
    gathered = lax.all_gather(packed, "tile", axis=0, tiled=True)
    sibling = lax.ppermute(gathered, "src", [(s, s ^ 1) for s in range(n_src)])
    head_parts = [head_weight] + [
        lax.ppermute(head_weight, "src", [(s, s ^ k) for s in range(n_src)]) for k in range(1, n_src)
    ]

    residual = tile_tokens.astype(jnp.float32)
    mean_square = jnp.mean(residual * residual, axis=1, keepdims=True)
    normed = (residual * lax.rsqrt(mean_square + 1e-05) * norm_gain).astype(jnp.bfloat16)

    def spread(x, rows, start):
        view = x.reshape(x.shape[0], n_tile, 2, rows // 2)
        pad = ((0, 0), (0, 0), (start, depth - start - rows // 2))
        mine = jnp.pad(lax.dynamic_index_in_dim(view, half, 2, keepdims=False), pad)
        other = jnp.pad(lax.dynamic_index_in_dim(view, 1 - half, 2, keepdims=False), pad)
        return mine.reshape(x.shape[0], -1), other.reshape(x.shape[0], -1)

    normed_mine, normed_other = spread(normed, up_rows, 0)
    pre_act = jnp.dot(normed_mine, gathered, preferred_element_type=jnp.float32) + jnp.dot(
        normed_other, sibling, preferred_element_type=jnp.float32
    )
    hidden = jax.nn.gelu(pre_act[:, :ff]).astype(jnp.bfloat16)
    hidden_mine, hidden_other = spread(hidden, down_rows, up_half)
    branch_out = jnp.dot(hidden_mine, gathered, preferred_element_type=jnp.float32) + jnp.dot(
        hidden_other, sibling, preferred_element_type=jnp.float32
    )
    branch_out = branch_out[:, :d_model]
    mixed = (residual + branch_out).astype(jnp.bfloat16)
    parts = jnp.stack(head_parts, 0)
    coeff_parts = jnp.einsum("tk,pkc->ptc", mixed, parts, preferred_element_type=jnp.float32).astype(
        jnp.bfloat16
    )
    order = me ^ jnp.arange(n_src, dtype=jnp.int32)
    coeffs = jnp.take(coeff_parts, order, axis=0).transpose(1, 0, 2).reshape(token_count, -1)
    tile_count = token_count // PATCH
    spec_rows = (
        coeffs.reshape(tile_count, GRID, GRID, 6, 2, SUB, SUB)
        .transpose(0, 1, 5, 3, 4, 6, 2)
        .reshape(tile_count, ORD, 12 * ORD)
    )
    return imaging(spec_rows, source_index, source_cutoff, source_weight)


def solution(mesh):
    return jax.shard_map(
        local,
        mesh=mesh,
        in_specs=(
            P(("tile", "src"), None),
            P(),
            P("tile", None),
            P("tile", None),
            P(None, "src"),
            P(),
            P(),
            P(),
        ),
        out_specs=P(("tile", "src"), None),
        check_vma=False,
    )
```

```python
import functools
import math

import jax
import jax.numpy as jnp
from jax import lax
from jax.experimental import pallas as pl
from jax.experimental.pallas import tpu as pltpu
from jax.sharding import PartitionSpec as P

GRID = 16
SUB = 8
W = 32
REG = 64
PIX = 64
SRC_DEV = 4
PATCH = 256
ORD = 128
f32 = jnp.float32
bf16 = jnp.bfloat16


def split_bf16(x):
    hi = lax.reduce_precision(x, exponent_bits=8, mantissa_bits=7)
    lo = x - hi
    return hi.astype(bf16), lo.astype(bf16)


def phase_tables():
    turn = 2.0 * math.pi / PIX
    v = jnp.arange(ORD, dtype=jnp.int32)
    y = jnp.arange(PIX, dtype=jnp.int32)
    ang = jnp.mod(v[:, None] * y[None, :], PIX).astype(f32) * turn
    cv, sv = jnp.cos(ang), jnp.sin(ang)
    t1 = jnp.concatenate([jnp.concatenate([cv, sv], 1), jnp.concatenate([-sv, cv], 1)], 0)
    i = jnp.arange(W, dtype=jnp.int32)
    x = jnp.arange(PIX, dtype=jnp.int32)
    ang2 = jnp.mod(x[:, None] * i[None, :], PIX).astype(f32) * turn
    t2 = jnp.concatenate([jnp.cos(ang2), jnp.sin(ang2)], 0)
    return t1, t2


def power_kernel(w_ref, x0_ref, y0_ref, r_ref, spec_ref, t1_ref, t2_ref, out_ref, xs, rcat, *, sb):
    step = pl.program_id(0)
    rcat[3 * W:, :] = jnp.zeros((W, sb * 6 * 2 * PIX), bf16)
    n = lax.broadcasted_iota(jnp.int32, (W, 2 * ORD), 1)
    col = (n % GRID) * SUB + (n % ORD) // GRID
    row = lax.broadcasted_iota(jnp.int32, (W, 2 * ORD), 0)
    keeps = []
    for j in range(sb):
        s = step * sb + j
        jj = col - y0_ref[s]
        radius = r_ref[s]
        keep = ((row - W // 2) ** 2 + (jj - W // 2) ** 2 <= radius * radius) & (jj >= 0) & (jj < W)
        keeps.append(keep)
    for k in range(6):
        for j in range(sb):
            s = step * sb + j
            start = x0_ref[s]
            base = pl.multiple_of((start // 8) * 8, 8)
            wide = spec_ref[pl.ds(base, W + 8), pl.ds(k * 2 * ORD, 2 * ORD)]
            rows = pltpu.roll(wide, (W + 8 - (start - base)) % (W + 8), 0)[:W]
            xs[j * W:(j + 1) * W, :] = jnp.where(keeps[j], rows, 0.0).astype(bf16)
        y = jnp.dot(xs[...], t1_ref[...], preferred_element_type=f32)
        h = y[:, : 2 * PIX] + y[:, 2 * PIX:]
        hh = h.astype(bf16)
        hl = (h - hh.astype(f32)).astype(bf16)
        for j in range(sb):
            m = k * sb + j
            cols = slice(m * 2 * PIX, (m + 1) * 2 * PIX)
            rows_ = slice(j * W, (j + 1) * W)
            rcat[0:W, cols] = hh[rows_, :]
            rcat[W:2 * W, cols] = hl[rows_, :]
            rcat[2 * W:3 * W, cols] = hh[rows_, :]
    q = jnp.dot(t2_ref[...], rcat[...], preferred_element_type=f32)
    acc = jnp.zeros((PIX, 2 * PIX), f32)
    for j in range(sb):
        part = jnp.zeros((PIX, 2 * PIX), f32)
        for k in range(6):
            m = k * sb + j
            blk = q[:, m * 2 * PIX:(m + 1) * 2 * PIX]
            rolled = pltpu.roll(blk, PIX, 1)
            er = blk[:PIX] - rolled[PIX:]
            ei = blk[PIX:] + rolled[:PIX]
            part = part + er * er + ei * ei
        acc = acc + w_ref[step * sb + j] * part

    @pl.when(step == 0)
    def _():
        out_ref[...] = jnp.zeros_like(out_ref)

    out_ref[...] += acc[:, :PIX]


def imaging(spec_rows, source_index, source_cutoff, source_weight, sb=32):
    T = spec_rows.shape[0]
    S = source_index.shape[0]
    x0 = jnp.clip(source_index[:, 0], 0, ORD - W)
    y0 = jnp.clip(source_index[:, 1], 0, ORD - W)
    t1, t2 = phase_tables()
    t1 = t1.reshape(2, GRID, SUB, 2 * PIX).transpose(0, 2, 1, 3).reshape(2 * ORD, 2 * PIX)
    t1h, t1l = split_bf16(t1)
    t1s = jnp.concatenate([t1h, t1l], 1)
    t2h, t2l = split_bf16(t2)
    t2c = jnp.concatenate([t2h, t2h, t2l, jnp.zeros((2 * PIX, W), bf16)], 1)
    smem = pl.BlockSpec(memory_space=pltpu.SMEM)
    call = pl.pallas_call(
        functools.partial(power_kernel, sb=sb),
        out_shape=jax.ShapeDtypeStruct((PIX, PIX), f32),
        grid=(S // sb,),
        in_specs=[smem] * 4
        + [
            pl.BlockSpec((ORD + 8, 12 * ORD), lambda s: (0, 0)),
            pl.BlockSpec((2 * ORD, 4 * PIX), lambda s: (0, 0)),
            pl.BlockSpec((2 * PIX, 4 * W), lambda s: (0, 0)),
        ],
        out_specs=pl.BlockSpec((PIX, PIX), lambda s: (0, 0)),
        scratch_shapes=[pltpu.VMEM((sb * W, 2 * ORD), bf16), pltpu.VMEM((4 * W, sb * 6 * 2 * PIX), bf16)],
        compiler_params=pltpu.CompilerParams(dimension_semantics=("arbitrary",)),
    )
    scaled = source_weight.astype(f32) * (1.0 / (6.0 * W * W * S))
    outs = []
    for t in range(T):
        outs.append(
            call(
                scaled, x0, y0, source_cutoff, jnp.pad(spec_rows[t].astype(f32), ((0, 8), (0, 0))), t1s, t2c
            )
        )
    power = jnp.stack(outs, 0)
    return power.reshape(T, PIX * PIX)


def local(
    tile_tokens,
    norm_gain,
    up_weight,
    down_weight,
    head_weight,
    source_index,
    source_cutoff,
    source_weight,
):
    token_count, d_model = tile_tokens.shape
    n_tile = lax.axis_size("tile")
    n_src = lax.axis_size("src")
    me = lax.axis_index("src")
    half = me % 2
    up_rows, ff = up_weight.shape
    down_rows = down_weight.shape[0]
    up_half, down_half = up_rows // 2, down_rows // 2
    depth = -(-(up_half + down_half) // 16) * 16
    width = max(ff, d_model)
    up_part = lax.dynamic_slice_in_dim(up_weight, half * up_half, up_half, 0)
    down_part = lax.dynamic_slice_in_dim(down_weight, half * down_half, down_half, 0)
    packed = jnp.concatenate(
        [
            jnp.pad(up_part, ((0, 0), (0, width - ff))),
            jnp.pad(down_part, ((0, depth - up_half - down_half), (0, width - d_model))),
        ],
        0,
    )
    gathered = lax.all_gather(packed, "tile", axis=0, tiled=True)
    sibling = lax.ppermute(gathered, "src", [(s, s ^ 1) for s in range(n_src)])
    head_parts = [head_weight] + [
        lax.ppermute(head_weight, "src", [(s, s ^ k) for s in range(n_src)]) for k in range(1, n_src)
    ]

    residual = tile_tokens.astype(jnp.float32)
    mean_square = jnp.mean(residual * residual, axis=1, keepdims=True)
    normed = (residual * lax.rsqrt(mean_square + 1e-05) * norm_gain).astype(jnp.bfloat16)

    def spread(x, rows, start):
        view = x.reshape(x.shape[0], n_tile, 2, rows // 2)
        pad = ((0, 0), (0, 0), (start, depth - start - rows // 2))
        mine = jnp.pad(lax.dynamic_index_in_dim(view, half, 2, keepdims=False), pad)
        other = jnp.pad(lax.dynamic_index_in_dim(view, 1 - half, 2, keepdims=False), pad)
        return mine.reshape(x.shape[0], -1), other.reshape(x.shape[0], -1)

    normed_mine, normed_other = spread(normed, up_rows, 0)
    pre_act = jnp.dot(normed_mine, gathered, preferred_element_type=jnp.float32) + jnp.dot(
        normed_other, sibling, preferred_element_type=jnp.float32
    )
    hidden = jax.nn.gelu(pre_act[:, :ff]).astype(jnp.bfloat16)
    hidden_mine, hidden_other = spread(hidden, down_rows, up_half)
    branch_out = jnp.dot(hidden_mine, gathered, preferred_element_type=jnp.float32) + jnp.dot(
        hidden_other, sibling, preferred_element_type=jnp.float32
    )
    branch_out = branch_out[:, :d_model]
    mixed = (residual + branch_out).astype(jnp.bfloat16)
    parts = jnp.stack(head_parts, 0)
    coeff_parts = jnp.einsum("tk,pkc->ptc", mixed, parts, preferred_element_type=jnp.float32).astype(
        jnp.bfloat16
    )
    order = me ^ jnp.arange(n_src, dtype=jnp.int32)
    coeffs = jnp.take(coeff_parts, order, axis=0).transpose(1, 0, 2).reshape(token_count, -1)
    tile_count = token_count // PATCH
    spec_rows = (
        coeffs.reshape(tile_count, GRID, GRID, 6, 2, SUB, SUB)
        .transpose(0, 1, 5, 3, 4, 6, 2)
        .reshape(tile_count, ORD, 12 * ORD)
    )
    return imaging(spec_rows, source_index, source_cutoff, source_weight)


def solution(mesh):
    return jax.shard_map(
        local,
        mesh=mesh,
        in_specs=(
            P(("tile", "src"), None),
            P(),
            P("tile", None),
            P("tile", None),
            P(None, "src"),
            P(),
            P(),
            P(),
        ),
        out_specs=P(("tile", "src"), None),
        check_vma=False,
    )
```

```python
import functools
import math

import jax
import jax.numpy as jnp
from jax import lax
from jax.experimental import pallas as pl
from jax.experimental.pallas import tpu as pltpu
from jax.sharding import PartitionSpec as P

GRID = 16
SUB = 8
W = 32
REG = 64
PIX = 64
SRC_DEV = 4
PATCH = 256
ORD = 128
f32 = jnp.float32
bf16 = jnp.bfloat16


def split_bf16(x):
    hi = lax.reduce_precision(x, exponent_bits=8, mantissa_bits=7)
    lo = x - hi
    return hi.astype(bf16), lo.astype(bf16)


def phase_tables():
    turn = 2.0 * math.pi / PIX
    v = jnp.arange(ORD, dtype=jnp.int32)
    y = jnp.arange(PIX, dtype=jnp.int32)
    ang = jnp.mod(v[:, None] * y[None, :], PIX).astype(f32) * turn
    cv, sv = jnp.cos(ang), jnp.sin(ang)
    t1 = jnp.concatenate([jnp.concatenate([cv, sv], 1), jnp.concatenate([-sv, cv], 1)], 0)
    i = jnp.arange(W, dtype=jnp.int32)
    x = jnp.arange(PIX, dtype=jnp.int32)
    ang2 = jnp.mod(x[:, None] * i[None, :], PIX).astype(f32) * turn
    t2 = jnp.concatenate([jnp.cos(ang2), jnp.sin(ang2)], 0)
    return t1, t2


def power_kernel(w_ref, x0_ref, y0_ref, r_ref, spec_ref, t1_ref, t2_ref, out_ref, xs, rcat, *, sb):
    step = pl.program_id(0)
    rcat[3 * W:, :] = jnp.zeros((W, sb * 6 * 2 * PIX), bf16)
    n = lax.broadcasted_iota(jnp.int32, (W, 2 * ORD), 1)
    col = (n % GRID) * SUB + (n % ORD) // GRID
    row = lax.broadcasted_iota(jnp.int32, (W, 2 * ORD), 0)
    keeps = []
    for j in range(sb):
        s = step * sb + j
        jj = col - y0_ref[s]
        radius = r_ref[s]
        keep = ((row - W // 2) ** 2 + (jj - W // 2) ** 2 <= radius * radius) & (jj >= 0) & (jj < W)
        keeps.append(keep)
    for k in range(6):
        for j in range(sb):
            s = step * sb + j
            start = x0_ref[s]
            base = pl.multiple_of((start // 8) * 8, 8)
            wide = spec_ref[pl.ds(base, W + 8), pl.ds(k * 2 * ORD, 2 * ORD)]
            rows = pltpu.roll(wide, (W + 8 - (start - base)) % (W + 8), 0)[:W]
            xs[j * W:(j + 1) * W, :] = jnp.where(keeps[j], rows, 0.0).astype(bf16)
        y = jnp.dot(xs[...], t1_ref[...], preferred_element_type=f32)
        h = y[:, : 2 * PIX] + y[:, 2 * PIX:]
        hh = h.astype(bf16)
        hl = (h - hh.astype(f32)).astype(bf16)
        for j in range(sb):
            m = k * sb + j
            cols = slice(m * 2 * PIX, (m + 1) * 2 * PIX)
            rows_ = slice(j * W, (j + 1) * W)
            rcat[0:W, cols] = hh[rows_, :]
            rcat[W:2 * W, cols] = hl[rows_, :]
            rcat[2 * W:3 * W, cols] = hh[rows_, :]
    q = jnp.dot(t2_ref[...], rcat[...], preferred_element_type=f32)
    acc = jnp.zeros((PIX, 2 * PIX), f32)
    for j in range(sb):
        part = jnp.zeros((PIX, 2 * PIX), f32)
        for k in range(6):
            m = k * sb + j
            blk = q[:, m * 2 * PIX:(m + 1) * 2 * PIX]
            rolled = pltpu.roll(blk, PIX, 1)
            er = blk[:PIX] - rolled[PIX:]
            ei = blk[PIX:] + rolled[:PIX]
            part = part + er * er + ei * ei
        acc = acc + w_ref[step * sb + j] * part

    @pl.when(step == 0)
    def _():
        out_ref[...] = jnp.zeros_like(out_ref)

    out_ref[...] += acc[:, :PIX]


def imaging(spec_rows, source_index, source_cutoff, source_weight, sb=32):
    T = spec_rows.shape[0]
    S = source_index.shape[0]
    x0 = jnp.clip(source_index[:, 0], 0, ORD - W)
    y0 = jnp.clip(source_index[:, 1], 0, ORD - W)
    t1, t2 = phase_tables()
    t1 = t1.reshape(2, GRID, SUB, 2 * PIX).transpose(0, 2, 1, 3).reshape(2 * ORD, 2 * PIX)
    t1h, t1l = split_bf16(t1)
    t1s = jnp.concatenate([t1h, t1l], 1)
    t2h, t2l = split_bf16(t2)
    t2c = jnp.concatenate([t2h, t2h, t2l, jnp.zeros((2 * PIX, W), bf16)], 1)
    smem = pl.BlockSpec(memory_space=pltpu.SMEM)
    call = pl.pallas_call(
        functools.partial(power_kernel, sb=sb),
        out_shape=jax.ShapeDtypeStruct((PIX, PIX), f32),
        grid=(S // sb,),
        in_specs=[smem] * 4
        + [
            pl.BlockSpec((ORD + 8, 12 * ORD), lambda s: (0, 0)),
            pl.BlockSpec((2 * ORD, 4 * PIX), lambda s: (0, 0)),
            pl.BlockSpec((2 * PIX, 4 * W), lambda s: (0, 0)),
        ],
        out_specs=pl.BlockSpec((PIX, PIX), lambda s: (0, 0)),
        scratch_shapes=[pltpu.VMEM((sb * W, 2 * ORD), bf16), pltpu.VMEM((4 * W, sb * 6 * 2 * PIX), bf16)],
        compiler_params=pltpu.CompilerParams(dimension_semantics=("arbitrary",)),
    )
    scaled = source_weight.astype(f32) * (1.0 / (6.0 * W * W * S))
    outs = []
    for t in range(T):
        outs.append(
            call(
                scaled, x0, y0, source_cutoff, jnp.pad(spec_rows[t].astype(f32), ((0, 8), (0, 0))), t1s, t2c
            )
        )
    power = jnp.stack(outs, 0)
    return power.reshape(T, PIX * PIX)


def local(
    tile_tokens,
    norm_gain,
    up_weight,
    down_weight,
    head_weight,
    source_index,
    source_cutoff,
    source_weight,
):
    token_count, d_model = tile_tokens.shape
    n_tile = lax.axis_size("tile")
    n_src = lax.axis_size("src")
    me = lax.axis_index("src")
    half = me % 2
    up_rows, ff = up_weight.shape
    down_rows = down_weight.shape[0]
    up_half, down_half = up_rows // 2, down_rows // 2
    depth = -(-(up_half + down_half) // 16) * 16
    width = max(ff, d_model)
    up_part = lax.dynamic_slice_in_dim(up_weight, half * up_half, up_half, 0)
    down_part = lax.dynamic_slice_in_dim(down_weight, half * down_half, down_half, 0)
    packed = jnp.concatenate(
        [
            jnp.pad(up_part, ((0, 0), (0, width - ff))),
            jnp.pad(down_part, ((0, depth - up_half - down_half), (0, width - d_model))),
        ],
        0,
    )
    gathered = lax.all_gather(packed, "tile", axis=0, tiled=True)
    sibling = lax.ppermute(gathered, "src", [(s, s ^ 1) for s in range(n_src)])
    head_parts = [head_weight] + [
        lax.ppermute(head_weight, "src", [(s, s ^ k) for s in range(n_src)]) for k in range(1, n_src)
    ]

    residual = tile_tokens.astype(jnp.float32)
    mean_square = jnp.mean(residual * residual, axis=1, keepdims=True)
    normed = (residual * lax.rsqrt(mean_square + 1e-05) * norm_gain).astype(jnp.bfloat16)

    def spread(x, rows, start):
        view = x.reshape(x.shape[0], n_tile, 2, rows // 2)
        pad = ((0, 0), (0, 0), (start, depth - start - rows // 2))
        mine = jnp.pad(lax.dynamic_index_in_dim(view, half, 2, keepdims=False), pad)
        other = jnp.pad(lax.dynamic_index_in_dim(view, 1 - half, 2, keepdims=False), pad)
        return mine.reshape(x.shape[0], -1), other.reshape(x.shape[0], -1)

    normed_mine, normed_other = spread(normed, up_rows, 0)
    pre_act = jnp.dot(normed_mine, gathered, preferred_element_type=jnp.float32) + jnp.dot(
        normed_other, sibling, preferred_element_type=jnp.float32
    )
    hidden = jax.nn.gelu(pre_act[:, :ff]).astype(jnp.bfloat16)
    hidden_mine, hidden_other = spread(hidden, down_rows, up_half)
    branch_out = jnp.dot(hidden_mine, gathered, preferred_element_type=jnp.float32) + jnp.dot(
        hidden_other, sibling, preferred_element_type=jnp.float32
    )
    branch_out = branch_out[:, :d_model]
    mixed = (residual + branch_out).astype(jnp.bfloat16)
    parts = jnp.stack(head_parts, 0)
    order = me ^ jnp.arange(n_src, dtype=jnp.int32)
    head_full = jnp.take(parts, order, axis=0).transpose(1, 0, 2).reshape(d_model, -1)
    coeffs = jnp.dot(mixed, head_full, preferred_element_type=jnp.float32).astype(jnp.bfloat16)
    tile_count = token_count // PATCH
    spec_rows = (
        coeffs.reshape(tile_count, GRID, GRID, 6, 2, SUB, SUB)
        .transpose(0, 1, 5, 3, 4, 6, 2)
        .reshape(tile_count, ORD, 12 * ORD)
    )
    return imaging(spec_rows, source_index, source_cutoff, source_weight)


def solution(mesh):
    return jax.shard_map(
        local,
        mesh=mesh,
        in_specs=(
            P(("tile", "src"), None),
            P(),
            P("tile", None),
            P("tile", None),
            P(None, "src"),
            P(),
            P(),
            P(),
        ),
        out_specs=P(("tile", "src"), None),
        check_vma=False,
    )
```

```python
import functools
import math

import jax
import jax.numpy as jnp
from jax import lax
from jax.experimental import pallas as pl
from jax.experimental.pallas import tpu as pltpu
from jax.sharding import PartitionSpec as P

GRID = 16
SUB = 8
W = 32
REG = 64
PIX = 64
SRC_DEV = 4
PATCH = 256
ORD = 128
f32 = jnp.float32
bf16 = jnp.bfloat16


def split_bf16(x):
    hi = lax.reduce_precision(x, exponent_bits=8, mantissa_bits=7)
    lo = x - hi
    return hi.astype(bf16), lo.astype(bf16)


def phase_tables():
    turn = 2.0 * math.pi / PIX
    v = jnp.arange(ORD, dtype=jnp.int32)
    y = jnp.arange(PIX, dtype=jnp.int32)
    ang = jnp.mod(v[:, None] * y[None, :], PIX).astype(f32) * turn
    cv, sv = jnp.cos(ang), jnp.sin(ang)
    t1 = jnp.concatenate([jnp.concatenate([cv, sv], 1), jnp.concatenate([-sv, cv], 1)], 0)
    i = jnp.arange(W, dtype=jnp.int32)
    x = jnp.arange(PIX, dtype=jnp.int32)
    ang2 = jnp.mod(x[:, None] * i[None, :], PIX).astype(f32) * turn
    t2 = jnp.concatenate([jnp.cos(ang2), jnp.sin(ang2)], 0)
    return t1, t2


def power_kernel(w_ref, x0_ref, y0_ref, r_ref, spec_ref, t1_ref, t2_ref, out_ref, xs, rcat, *, sb):
    step = pl.program_id(0)
    rcat[3 * W:, :] = jnp.zeros((W, sb * 6 * 2 * PIX), bf16)
    n = lax.broadcasted_iota(jnp.int32, (W, 2 * ORD), 1)
    col = (n % GRID) * SUB + (n % ORD) // GRID
    row = lax.broadcasted_iota(jnp.int32, (W, 2 * ORD), 0)
    keeps = []
    for j in range(sb):
        s = step * sb + j
        jj = col - y0_ref[s]
        radius = r_ref[s]
        keep = ((row - W // 2) ** 2 + (jj - W // 2) ** 2 <= radius * radius) & (jj >= 0) & (jj < W)
        keeps.append(keep)
    for k in range(6):
        for j in range(sb):
            s = step * sb + j
            start = x0_ref[s]
            base = pl.multiple_of(jnp.minimum((start // 8) * 8, ORD - W - 8), 8)
            wide = spec_ref[pl.ds(base, W + 8), pl.ds(k * 2 * ORD, 2 * ORD)]
            rows = pltpu.roll(wide, (W + 8 - (start - base)) % (W + 8), 0)[:W]
            xs[j * W:(j + 1) * W, :] = jnp.where(keeps[j], rows, 0.0).astype(bf16)
        y = jnp.dot(xs[...], t1_ref[...], preferred_element_type=f32)
        h = y[:, : 2 * PIX] + y[:, 2 * PIX:]
        hh = h.astype(bf16)
        hl = (h - hh.astype(f32)).astype(bf16)
        for j in range(sb):
            m = k * sb + j
            cols = slice(m * 2 * PIX, (m + 1) * 2 * PIX)
            rows_ = slice(j * W, (j + 1) * W)
            rcat[0:W, cols] = hh[rows_, :]
            rcat[W:2 * W, cols] = hl[rows_, :]
            rcat[2 * W:3 * W, cols] = hh[rows_, :]
    q = jnp.dot(t2_ref[...], rcat[...], preferred_element_type=f32)
    acc = jnp.zeros((PIX, 2 * PIX), f32)
    for j in range(sb):
        part = jnp.zeros((PIX, 2 * PIX), f32)
        for k in range(6):
            m = k * sb + j
            blk = q[:, m * 2 * PIX:(m + 1) * 2 * PIX]
            rolled = pltpu.roll(blk, PIX, 1)
            er = blk[:PIX] - rolled[PIX:]
            ei = blk[PIX:] + rolled[:PIX]
            part = part + er * er + ei * ei
        acc = acc + w_ref[step * sb + j] * part

    @pl.when(step == 0)
    def _():
        out_ref[...] = jnp.zeros_like(out_ref)

    out_ref[...] += acc[:, :PIX]


def imaging(spec_rows, source_index, source_cutoff, source_weight, sb=32):
    T = spec_rows.shape[0]
    S = source_index.shape[0]
    x0 = jnp.clip(source_index[:, 0], 0, ORD - W)
    y0 = jnp.clip(source_index[:, 1], 0, ORD - W)
    t1, t2 = phase_tables()
    t1 = t1.reshape(2, GRID, SUB, 2 * PIX).transpose(0, 2, 1, 3).reshape(2 * ORD, 2 * PIX)
    t1h, t1l = split_bf16(t1)
    t1s = jnp.concatenate([t1h, t1l], 1)
    t2h, t2l = split_bf16(t2)
    t2c = jnp.concatenate([t2h, t2h, t2l, jnp.zeros((2 * PIX, W), bf16)], 1)
    smem = pl.BlockSpec(memory_space=pltpu.SMEM)
    call = pl.pallas_call(
        functools.partial(power_kernel, sb=sb),
        out_shape=jax.ShapeDtypeStruct((PIX, PIX), f32),
        grid=(S // sb,),
        in_specs=[smem] * 4
        + [
            pl.BlockSpec((ORD, 12 * ORD), lambda s: (0, 0)),
            pl.BlockSpec((2 * ORD, 4 * PIX), lambda s: (0, 0)),
            pl.BlockSpec((2 * PIX, 4 * W), lambda s: (0, 0)),
        ],
        out_specs=pl.BlockSpec((PIX, PIX), lambda s: (0, 0)),
        scratch_shapes=[pltpu.VMEM((sb * W, 2 * ORD), bf16), pltpu.VMEM((4 * W, sb * 6 * 2 * PIX), bf16)],
        compiler_params=pltpu.CompilerParams(dimension_semantics=("arbitrary",)),
    )
    scaled = source_weight.astype(f32) * (1.0 / (6.0 * W * W * S))
    outs = []
    for t in range(T):
        outs.append(
            call(
                scaled, x0, y0, source_cutoff, spec_rows[t].astype(f32), t1s, t2c
            )
        )
    power = jnp.stack(outs, 0)
    return power.reshape(T, PIX * PIX)


def local(
    tile_tokens,
    norm_gain,
    up_weight,
    down_weight,
    head_weight,
    source_index,
    source_cutoff,
    source_weight,
):
    token_count, d_model = tile_tokens.shape
    n_tile = lax.axis_size("tile")
    n_src = lax.axis_size("src")
    me = lax.axis_index("src")
    half = me % 2
    up_rows, ff = up_weight.shape
    down_rows = down_weight.shape[0]
    up_half, down_half = up_rows // 2, down_rows // 2
    depth = -(-(up_half + down_half) // 16) * 16
    width = max(ff, d_model)
    up_part = lax.dynamic_slice_in_dim(up_weight, half * up_half, up_half, 0)
    down_part = lax.dynamic_slice_in_dim(down_weight, half * down_half, down_half, 0)
    packed = jnp.concatenate(
        [
            jnp.pad(up_part, ((0, 0), (0, width - ff))),
            jnp.pad(down_part, ((0, depth - up_half - down_half), (0, width - d_model))),
        ],
        0,
    )
    gathered = lax.all_gather(packed, "tile", axis=0, tiled=True)
    sibling = lax.ppermute(gathered, "src", [(s, s ^ 1) for s in range(n_src)])
    head_parts = [head_weight] + [
        lax.ppermute(head_weight, "src", [(s, s ^ k) for s in range(n_src)]) for k in range(1, n_src)
    ]

    residual = tile_tokens.astype(jnp.float32)
    mean_square = jnp.mean(residual * residual, axis=1, keepdims=True)
    normed = (residual * lax.rsqrt(mean_square + 1e-05) * norm_gain).astype(jnp.bfloat16)

    def spread(x, rows, start):
        view = x.reshape(x.shape[0], n_tile, 2, rows // 2)
        pad = ((0, 0), (0, 0), (start, depth - start - rows // 2))
        mine = jnp.pad(lax.dynamic_index_in_dim(view, half, 2, keepdims=False), pad)
        other = jnp.pad(lax.dynamic_index_in_dim(view, 1 - half, 2, keepdims=False), pad)
        return mine.reshape(x.shape[0], -1), other.reshape(x.shape[0], -1)

    normed_mine, normed_other = spread(normed, up_rows, 0)
    pre_act = jnp.dot(normed_mine, gathered, preferred_element_type=jnp.float32) + jnp.dot(
        normed_other, sibling, preferred_element_type=jnp.float32
    )
    hidden = jax.nn.gelu(pre_act[:, :ff]).astype(jnp.bfloat16)
    hidden_mine, hidden_other = spread(hidden, down_rows, up_half)
    branch_out = jnp.dot(hidden_mine, gathered, preferred_element_type=jnp.float32) + jnp.dot(
        hidden_other, sibling, preferred_element_type=jnp.float32
    )
    branch_out = branch_out[:, :d_model]
    mixed = (residual + branch_out).astype(jnp.bfloat16)
    parts = jnp.stack(head_parts, 0)
    coeff_parts = jnp.einsum("tk,pkc->ptc", mixed, parts, preferred_element_type=jnp.float32).astype(
        jnp.bfloat16
    )
    order = me ^ jnp.arange(n_src, dtype=jnp.int32)
    coeffs = jnp.take(coeff_parts, order, axis=0).transpose(1, 0, 2).reshape(token_count, -1)
    tile_count = token_count // PATCH
    spec_rows = (
        coeffs.reshape(tile_count, GRID, GRID, 6, 2, SUB, SUB)
        .transpose(0, 1, 5, 3, 4, 6, 2)
        .reshape(tile_count, ORD, 12 * ORD)
    )
    return imaging(spec_rows, source_index, source_cutoff, source_weight)


def solution(mesh):
    return jax.shard_map(
        local,
        mesh=mesh,
        in_specs=(
            P(("tile", "src"), None),
            P(),
            P("tile", None),
            P("tile", None),
            P(None, "src"),
            P(),
            P(),
            P(),
        ),
        out_specs=P(("tile", "src"), None),
        check_vma=False,
    )
```

```python
import functools
import math

import jax
import jax.numpy as jnp
from jax import lax
from jax.experimental import pallas as pl
from jax.experimental.pallas import tpu as pltpu
from jax.sharding import PartitionSpec as P

GRID = 16
SUB = 8
W = 32
REG = 64
PIX = 64
SRC_DEV = 4
PATCH = 256
ORD = 128
f32 = jnp.float32
bf16 = jnp.bfloat16


def split_bf16(x):
    hi = lax.reduce_precision(x, exponent_bits=8, mantissa_bits=7)
    lo = x - hi
    return hi.astype(bf16), lo.astype(bf16)


def phase_tables():
    turn = 2.0 * math.pi / PIX
    v = jnp.arange(ORD, dtype=jnp.int32)
    y = jnp.arange(PIX, dtype=jnp.int32)
    ang = jnp.mod(v[:, None] * y[None, :], PIX).astype(f32) * turn
    cv, sv = jnp.cos(ang), jnp.sin(ang)
    t1 = jnp.concatenate([jnp.concatenate([cv, sv], 1), jnp.concatenate([-sv, cv], 1)], 0)
    i = jnp.arange(W, dtype=jnp.int32)
    x = jnp.arange(PIX, dtype=jnp.int32)
    ang2 = jnp.mod(x[:, None] * i[None, :], PIX).astype(f32) * turn
    t2 = jnp.concatenate([jnp.cos(ang2), jnp.sin(ang2)], 0)
    return t1, t2


def power_kernel(w_ref, x0_ref, y0_ref, r_ref, spec_ref, t1_ref, t2_ref, out_ref, xs, rcat, *, sb):
    step = pl.program_id(0)
    rcat[3 * W:, :] = jnp.zeros((W, sb * 6 * 2 * PIX), bf16)
    n = lax.broadcasted_iota(jnp.int32, (W, 2 * ORD), 1)
    col = (n % GRID) * SUB + (n % ORD) // GRID
    row = lax.broadcasted_iota(jnp.int32, (W, 2 * ORD), 0)
    keeps = []
    for j in range(sb):
        s = step * sb + j
        jj = col - y0_ref[s]
        radius = r_ref[s]
        keep = ((row - W // 2) ** 2 + (jj - W // 2) ** 2 <= radius * radius) & (jj >= 0) & (jj < W)
        keeps.append(keep)
    for k in range(6):
        for j in range(sb):
            s = step * sb + j
            start = x0_ref[s]
            base = pl.multiple_of((start // 8) * 8, 8)
            wide = spec_ref[pl.ds(base, W + 8), pl.ds(k * 2 * ORD, 2 * ORD)]
            rows = pltpu.roll(wide, (W + 8 - (start - base)) % (W + 8), 0)[:W]
            xs[j * W:(j + 1) * W, :] = jnp.where(keeps[j], rows, 0.0).astype(bf16)
        y = jnp.dot(xs[...], t1_ref[...], preferred_element_type=f32)
        h = y[:, : 2 * PIX] + y[:, 2 * PIX:]
        hh = h.astype(bf16)
        hl = (h - hh.astype(f32)).astype(bf16)
        for j in range(sb):
            m = k * sb + j
            cols = slice(m * 2 * PIX, (m + 1) * 2 * PIX)
            rows_ = slice(j * W, (j + 1) * W)
            rcat[0:W, cols] = hh[rows_, :]
            rcat[W:2 * W, cols] = hl[rows_, :]
            rcat[2 * W:3 * W, cols] = hh[rows_, :]
    q = jnp.dot(t2_ref[...], rcat[...], preferred_element_type=f32)
    acc = jnp.zeros((PIX, 2 * PIX), f32)
    for j in range(sb):
        part = jnp.zeros((PIX, 2 * PIX), f32)
        for k in range(6):
            m = k * sb + j
            blk = q[:, m * 2 * PIX:(m + 1) * 2 * PIX]
            rolled = pltpu.roll(blk, PIX, 1)
            er = blk[:PIX] - rolled[PIX:]
            ei = blk[PIX:] + rolled[:PIX]
            part = part + er * er + ei * ei
        acc = acc + w_ref[step * sb + j] * part

    @pl.when(step == 0)
    def _():
        out_ref[...] = jnp.zeros_like(out_ref)

    out_ref[...] += acc[:, :PIX]


def imaging(spec_rows, source_index, source_cutoff, source_weight, sb=64):
    T = spec_rows.shape[0]
    S = source_index.shape[0]
    x0 = jnp.clip(source_index[:, 0], 0, ORD - W)
    y0 = jnp.clip(source_index[:, 1], 0, ORD - W)
    t1, t2 = phase_tables()
    t1 = t1.reshape(2, GRID, SUB, 2 * PIX).transpose(0, 2, 1, 3).reshape(2 * ORD, 2 * PIX)
    t1h, t1l = split_bf16(t1)
    t1s = jnp.concatenate([t1h, t1l], 1)
    t2h, t2l = split_bf16(t2)
    t2c = jnp.concatenate([t2h, t2h, t2l, jnp.zeros((2 * PIX, W), bf16)], 1)
    smem = pl.BlockSpec(memory_space=pltpu.SMEM)
    call = pl.pallas_call(
        functools.partial(power_kernel, sb=sb),
        out_shape=jax.ShapeDtypeStruct((PIX, PIX), f32),
        grid=(S // sb,),
        in_specs=[smem] * 4
        + [
            pl.BlockSpec((ORD + 8, 12 * ORD), lambda s: (0, 0)),
            pl.BlockSpec((2 * ORD, 4 * PIX), lambda s: (0, 0)),
            pl.BlockSpec((2 * PIX, 4 * W), lambda s: (0, 0)),
        ],
        out_specs=pl.BlockSpec((PIX, PIX), lambda s: (0, 0)),
        scratch_shapes=[pltpu.VMEM((sb * W, 2 * ORD), bf16), pltpu.VMEM((4 * W, sb * 6 * 2 * PIX), bf16)],
        compiler_params=pltpu.CompilerParams(dimension_semantics=("arbitrary",)),
    )
    scaled = source_weight.astype(f32) * (1.0 / (6.0 * W * W * S))
    outs = []
    for t in range(T):
        outs.append(
            call(
                scaled, x0, y0, source_cutoff, jnp.pad(spec_rows[t].astype(f32), ((0, 8), (0, 0))), t1s, t2c
            )
        )
    power = jnp.stack(outs, 0)
    return power.reshape(T, PIX * PIX)


def local(
    tile_tokens,
    norm_gain,
    up_weight,
    down_weight,
    head_weight,
    source_index,
    source_cutoff,
    source_weight,
):
    token_count, d_model = tile_tokens.shape
    n_tile = lax.axis_size("tile")
    n_src = lax.axis_size("src")
    me = lax.axis_index("src")
    half = me % 2
    up_rows, ff = up_weight.shape
    down_rows = down_weight.shape[0]
    up_half, down_half = up_rows // 2, down_rows // 2
    depth = -(-(up_half + down_half) // 16) * 16
    width = max(ff, d_model)
    up_part = lax.dynamic_slice_in_dim(up_weight, half * up_half, up_half, 0)
    down_part = lax.dynamic_slice_in_dim(down_weight, half * down_half, down_half, 0)
    packed = jnp.concatenate(
        [
            jnp.pad(up_part, ((0, 0), (0, width - ff))),
            jnp.pad(down_part, ((0, depth - up_half - down_half), (0, width - d_model))),
        ],
        0,
    )
    gathered = lax.all_gather(packed, "tile", axis=0, tiled=True)
    sibling = lax.ppermute(gathered, "src", [(s, s ^ 1) for s in range(n_src)])
    head_parts = [head_weight] + [
        lax.ppermute(head_weight, "src", [(s, s ^ k) for s in range(n_src)]) for k in range(1, n_src)
    ]

    residual = tile_tokens.astype(jnp.float32)
    mean_square = jnp.mean(residual * residual, axis=1, keepdims=True)
    normed = (residual * lax.rsqrt(mean_square + 1e-05) * norm_gain).astype(jnp.bfloat16)

    def spread(x, rows, start):
        view = x.reshape(x.shape[0], n_tile, 2, rows // 2)
        pad = ((0, 0), (0, 0), (start, depth - start - rows // 2))
        mine = jnp.pad(lax.dynamic_index_in_dim(view, half, 2, keepdims=False), pad)
        other = jnp.pad(lax.dynamic_index_in_dim(view, 1 - half, 2, keepdims=False), pad)
        return mine.reshape(x.shape[0], -1), other.reshape(x.shape[0], -1)

    normed_mine, normed_other = spread(normed, up_rows, 0)
    pre_act = jnp.dot(normed_mine, gathered, preferred_element_type=jnp.float32) + jnp.dot(
        normed_other, sibling, preferred_element_type=jnp.float32
    )
    hidden = jax.nn.gelu(pre_act[:, :ff]).astype(jnp.bfloat16)
    hidden_mine, hidden_other = spread(hidden, down_rows, up_half)
    branch_out = jnp.dot(hidden_mine, gathered, preferred_element_type=jnp.float32) + jnp.dot(
        hidden_other, sibling, preferred_element_type=jnp.float32
    )
    branch_out = branch_out[:, :d_model]
    mixed = (residual + branch_out).astype(jnp.bfloat16)
    parts = jnp.stack(head_parts, 0)
    coeff_parts = jnp.einsum("tk,pkc->ptc", mixed, parts, preferred_element_type=jnp.float32).astype(
        jnp.bfloat16
    )
    order = me ^ jnp.arange(n_src, dtype=jnp.int32)
    coeffs = jnp.take(coeff_parts, order, axis=0).transpose(1, 0, 2).reshape(token_count, -1)
    tile_count = token_count // PATCH
    spec_rows = (
        coeffs.reshape(tile_count, GRID, GRID, 6, 2, SUB, SUB)
        .transpose(0, 1, 5, 3, 4, 6, 2)
        .reshape(tile_count, ORD, 12 * ORD)
    )
    return imaging(spec_rows, source_index, source_cutoff, source_weight)


def solution(mesh):
    return jax.shard_map(
        local,
        mesh=mesh,
        in_specs=(
            P(("tile", "src"), None),
            P(),
            P("tile", None),
            P("tile", None),
            P(None, "src"),
            P(),
            P(),
            P(),
        ),
        out_specs=P(("tile", "src"), None),
        check_vma=False,
    )
```
